256 devices in a mesh: mem: 4 (over x), col: 64 (over y, z, core).
Axes of the slice: x: 4, y: 4, z: 8, core: 2. Of those that a mesh axis runs over, the one named last changes fastest.
Arguments:
- perturbations: bfloat16 [32, 256, 256, 128], P('mem', 'col'), may hold values from -4 to 4
- static_root: float32 [128, 128], replicated, may hold values from -0.5 to 1.5
- obs_jacobian: float32 [128, 128], replicated, may hold values from -0.5 to 0.5
- innovations: float32 [16384, 128], P('col'), may hold values from -6 to 6
- obs_weights: float32 [128], replicated, may hold values from 0.2 to 2
- length_scale: float32 [256, 256], P('col'), may hold values from 0.05 to 0.24
- obs_owner: int32 [16384, 1], P('col'), may hold values from 0 to 63; in each aligned block of 256 rows (0 to 255, 256 to 511, ...) at most 8 rows name the same one
- obs_cell: int32 [16384], P('col'), may hold values from 0 to 1023
- obs_count: int32 [64], P('col'), may hold values from 128 to 256, as said below
Outputs:
- increment: float32 [256, 256, 128], P('col', 'mem')
- control_static: float32 [256, 256, 128], P('col', 'mem')
- control_ensemble: float32 [32, 256, 256], P('mem', 'col')
The draws below stay inside these ranges and needn't reach their ends.
Inputs may be any that keep to these rules, and one draw needn't show every extreme that they name: `obs_owner`: each holder's 256 rows name any one column block at most 8 times. `obs_count`: rows at or past a holder's count are padding and are ignored; at least one holder is full. `obs_cell`: the column within the owner's block, numbered y * 256 + x, where y is its grid row within the block (0 to 3).
All inputs are finite; a program needn't handle non-finite values.
Results may differ from the reference program's by a relative error of at most 0.004.
Values may be sent and summed in bfloat16 or wider, within the bound.
No kernel may reach another device: no remote copies, remote signals or barrier semaphores. Data moves between devices by JAX's collectives and lax.ppermute only.
A program may use at most 64 MiB of HBM per device.

```python
import math
import jax
import jax.numpy as jnp
import numpy as np
from jax import lax

FEAT = 128
CH = 128
MEMBERS = 32
CY = 4
NX = 256
NY = 256
OBS_DEV = 256
OBS_TOT = 16384
CAP = 8
NSWEEP = 4
ITERS = 2
N_COL = 64


def draw_static_root(key, part):
    first, second = jax.random.split(jax.random.fold_in(key, 11))
    diagonal = jax.random.uniform(first, (FEAT,), jnp.float32, 0.7, 1.3)
    spread = jnp.clip(jax.random.normal(second, (FEAT, FEAT), jnp.float32), -4.0, 4.0) * (0.5 / math.sqrt(FEAT))
    return jnp.eye(FEAT, dtype=jnp.float32) * diagonal[None, :] + spread


def draw_obs_count(key, part):
    first, second = jax.random.split(jax.random.fold_in(key, 23))
    counts = jax.random.randint(first, (N_COL,), OBS_DEV // 2, OBS_DEV + 1)
    full_holder = jax.random.randint(second, (), 0, N_COL)
    return jnp.where(jnp.arange(N_COL) == full_holder, OBS_DEV, counts).astype(jnp.int32)


def touch_ends(drawn, own_key, least, largest):
    extent = drawn.shape
    place = [jax.random.randint(jax.random.fold_in(own_key, axis), (), 0, extent[axis]) for axis in range(len(extent))]
    drawn = drawn.at[tuple(place)].set(least)
    longest = extent.index(max(extent))
    place[longest] = (place[longest] + 1) % extent[longest]
    return drawn.at[tuple(place)].set(largest)


def levels(key, extent, pieces, smallest, largest):
    loudness = 1.0
    for axis_at, parts in pieces:
        heights = jax.random.uniform(jax.random.fold_in(jax.random.fold_in(key, 6), axis_at), (parts,), jnp.float32, smallest / len(pieces), largest / len(pieces))
        loudness = loudness * jnp.repeat(jnp.exp(heights), extent[axis_at] // parts).reshape((-1,) + (1,) * (len(extent) - 1 - axis_at))
    return loudness


def routed_block(stream_key, own, number, rows, count, top, most, lean):
    sequence = jax.random.permutation(stream_key, count)
    packed, common = portions_of(count, rows * top, most, lean, True), portions_of(count, rows * top, most, lean, False)
    places = jnp.arange(count)

    def named(lengths, rotation):
        used = int((lengths > 0).sum())
        fixed = max(1, used // 4)
        shifted = fixed + (places - fixed + rotation * (used - fixed)) % max(1, count - fixed)
        return jnp.zeros((count,), jnp.int32).at[sequence[jnp.where(places < fixed, places, shifted)]].set(jnp.asarray(lengths, jnp.int32))

    lengths = jnp.where(number % 4 == 0, named(packed, number // 4), named(common, number - number // 4 - 1))
    mixed = jax.random.permutation(jax.random.fold_in(own, 3), count)
    giver, taker = mixed[0:count // 2 * 2:2], mixed[1:count // 2 * 2:2]
    room = jnp.minimum(lengths[giver] - 1, most - lengths[taker]) // 2
    room = jnp.where((giver == sequence[0]) | (taker == sequence[0]) | (lengths[taker] == 0), 0, jnp.maximum(room, 0))
    shifted = jax.random.randint(jax.random.fold_in(own, 4), (count // 2,), 0, 1 << 20) % (room + 1)
    lengths = lengths.at[giver].add(-shifted).at[taker].add(shifted)
    items = jnp.searchsorted(jnp.cumsum(lengths), jnp.arange(rows * top), side="right").astype(jnp.int32)
    listing = items.reshape(top, rows).T
    listing = listing[jax.random.permutation(jax.random.fold_in(own, 1), rows)]
    rotation = jax.random.randint(jax.random.fold_in(own, 2), (rows, 1), 0, top)
    return jnp.take_along_axis(listing, (jnp.arange(top)[None, :] + rotation) % top, axis=1)


def portions_of(count, total, bound, slope, full):
    loads = [(1 << 20) // math.isqrt(grade ** slope) + 1 for grade in range(1, count + 1)]
    largest = bound if full else min(bound, max(-(-total // count), total * loads[0] // sum(loads)))
    least = 1 if total - largest >= count - 1 else 0
    holding, rest = [largest] + [least] * (count - 1), total - largest - least * (count - 1)
    while rest > 0:
        free = [i for i in range(1, count) if holding[i] < largest] or [i for i in range(1, count) if holding[i] < bound]
        pool, left = sum([loads[i] for i in free]), rest
        for i in free:
            extra = min(bound - holding[i], max(1, left * loads[i] // pool), rest)
            holding[i] = holding[i] + extra
            rest = rest - extra
    return np.array(holding)


def normal_values(key, shape, scale, most, cuts=(), kind=jnp.bfloat16):
    entries = scale * jax.random.normal(key, shape, jnp.float32)
    if cuts:
        entries = entries * levels(key, shape, cuts, -0.22, 0.18)
    return jnp.clip(entries, -most, most).astype(kind)


def setup_inputs(seed: int = 0) -> dict:
    streams_of = jax.random.split(jax.random.key(seed), 10)
    perturbations = normal_values(streams_of[0], (MEMBERS, NY, NX, FEAT), 0.3, 4.0, ((0, 4), (1, 64)))
    static_root = draw_static_root(jax.random.fold_in(streams_of[9], 71), 0)
    obs_jacobian = normal_values(streams_of[2], (FEAT, CH), FEAT ** -0.5, 0.5, (), jnp.float32)
    innovations = normal_values(streams_of[3], (OBS_TOT, CH), 1.0, 6.0, ((0, 64),), jnp.float32)
    obs_weights = jnp.clip(jnp.exp(jax.random.uniform(streams_of[4], (CH,), jnp.float32, math.log(0.2), math.log(2.0))), 0.2, 2.0)
    length_scale = jnp.clip(0.05 + 0.19 * jax.random.uniform(streams_of[5], (NY, NX), jnp.float32) ** levels(streams_of[5], (NY, NX), ((0, 64),), -0.2, 0.2), 0.05, 0.24)
    obs_owner_keys = jax.random.split(jax.random.fold_in(streams_of[6], 1), OBS_TOT // OBS_DEV)
    obs_owner_turns = jax.random.permutation(jax.random.fold_in(streams_of[6], 3), OBS_TOT // OBS_DEV)
    obs_owner = jax.vmap(lambda own, number: routed_block(jax.random.fold_in(streams_of[6], 2), own, number, OBS_DEV, N_COL, 1, CAP, 2))(obs_owner_keys, obs_owner_turns).reshape((OBS_TOT, 1))
    obs_cell = touch_ends(jax.random.randint(streams_of[7], (OBS_TOT,), 0, CY * NX), jax.random.fold_in(streams_of[7], 1), 0, (CY * NX) - 1).astype(jnp.int32)
    obs_count = draw_obs_count(jax.random.fold_in(streams_of[9], 71), 0)
    return dict(perturbations=perturbations, static_root=static_root, obs_jacobian=obs_jacobian, innovations=innovations, obs_weights=obs_weights, length_scale=length_scale, obs_owner=obs_owner, obs_cell=obs_cell, obs_count=obs_count)


def face_coefficients(length_scale):
    padded = jnp.pad(length_scale, 1)
    return (jnp.sqrt(length_scale * padded[:-2, 1:-1]), jnp.sqrt(length_scale * padded[2:, 1:-1]), jnp.sqrt(length_scale * padded[1:-1, :-2]), jnp.sqrt(length_scale * padded[1:-1, 2:]))

def sweeps(values, coeffs):
    face_up, face_down, face_left, face_right = coeffs
    for sweep_step in range(NSWEEP):
        padded = jnp.pad(values, ((0, 0), (1, 1), (1, 1)))
        centre = values
        values = centre + face_up * (padded[:, :-2, 1:-1] - centre) + face_down * (padded[:, 2:, 1:-1] - centre) + face_left * (padded[:, 1:-1, :-2] - centre) + face_right * (padded[:, 1:-1, 2:] - centre)
    return values

def forward_map(perturbations, static_root, coeffs, static_part, ensemble_part):
    smoothed = lax.optimization_barrier(sweeps(ensemble_part, coeffs).astype(jnp.bfloat16))

    def add_member(total, pair):
        member, weight = pair
        return (total + member.astype(jnp.float32) * weight.astype(jnp.float32)[:, :, None], None)
    total, unused = lax.scan(add_member, jnp.zeros((NY, NX, FEAT), jnp.float32), (perturbations, smoothed))
    static = jnp.dot(static_part.reshape(NY * NX, FEAT), static_root, precision=lax.Precision.HIGHEST).reshape(NY, NX, FEAT)
    return total + static

def adjoint_map(perturbations, static_root, coeffs, gradient):
    static = jnp.dot(gradient.reshape(NY * NX, FEAT), static_root.T, precision=lax.Precision.HIGHEST).reshape(NY, NX, FEAT)
    rounded = lax.optimization_barrier(gradient.astype(jnp.bfloat16)).astype(jnp.float32)
    projected = lax.map(lambda member: lax.optimization_barrier(jnp.sum(member.astype(jnp.float32) * rounded, axis=-1)), perturbations)
    return (static, sweeps(projected, coeffs))

def reference(perturbations, static_root, obs_jacobian, innovations, obs_weights, length_scale, obs_owner, obs_cell, obs_count):
    coeffs = face_coefficients(length_scale)
    positions = jnp.arange(OBS_TOT, dtype=jnp.int32)
    live = (positions % OBS_DEV < obs_count[positions // OBS_DEV]).astype(jnp.float32)
    flat_index = (obs_owner[:, 0] * (CY * NX) + obs_cell).astype(jnp.int32)
    obs_gain = live[:, None] * obs_weights[None, :]

    def spread_back(weighted):
        back = jnp.dot(weighted, obs_jacobian.T, precision=lax.Precision.HIGHEST)
        return jnp.zeros((NY * NX, FEAT), jnp.float32).at[flat_index].add(back).reshape(NY, NX, FEAT)

    def obs_hessian(image_part):
        gathered = image_part.reshape(NY * NX, FEAT)[flat_index]
        model_obs = jnp.dot(gathered, obs_jacobian, precision=lax.Precision.HIGHEST)
        return spread_back(obs_gain * model_obs)

    def inner(first, second):
        return jnp.sum(first[0] * second[0]) + jnp.sum(first[1] * second[1])
    residual = adjoint_map(perturbations, static_root, coeffs, spread_back(obs_gain * innovations))
    direction = residual
    state = (jnp.zeros((NY, NX, FEAT), jnp.float32), jnp.zeros((MEMBERS, NY, NX), jnp.float32))
    increment = jnp.zeros((NY, NX, FEAT), jnp.float32)
    norm_now = inner(residual, residual)
    for iteration in range(ITERS):
        image_part = forward_map(perturbations, static_root, coeffs, direction[0], direction[1])
        adj_static, adj_ensemble = adjoint_map(perturbations, static_root, coeffs, obs_hessian(image_part))
        image = (direction[0] + adj_static, direction[1] + adj_ensemble)
        step = norm_now / inner(direction, image)
        state = (state[0] + step * direction[0], state[1] + step * direction[1])
        residual = (residual[0] - step * image[0], residual[1] - step * image[1])
        increment = increment + step * image_part
        norm_next = inner(residual, residual)
        ratio = norm_next / norm_now
        direction = (residual[0] + ratio * direction[0], residual[1] + ratio * direction[1])
        norm_now = norm_next
    return (increment, state[0], state[1])
```

```python
import jax
import jax.numpy as jnp
from jax import lax
from jax.sharding import PartitionSpec as P

NSWEEP = 4
ITERS = 2


def neighbours(block, axis, dim):
    count = lax.axis_size(axis)
    forward = [(i, i + 1) for i in range(count - 1)]
    backward = [(target, source) for source, target in forward]
    low = lax.ppermute(block, axis, forward)
    high = lax.ppermute(block, axis, backward)
    return jnp.concatenate([low, block, high], axis=dim)


def face_coefficients(length_scale):
    rimmed = neighbours(length_scale, "col", 0)
    padded = jnp.pad(rimmed, ((1, 1), (1, 1)))
    centre = padded[1:-1, 1:-1]
    return (
        jnp.sqrt(centre * padded[:-2, 1:-1]),
        jnp.sqrt(centre * padded[2:, 1:-1]),
        jnp.sqrt(centre * padded[1:-1, :-2]),
        jnp.sqrt(centre * padded[1:-1, 2:]),
    )


def sweeps(values, coeffs):
    rows = values.shape[1]
    face_up, face_down, face_left, face_right = coeffs
    values = neighbours(values, "col", 1)
    for sweep_step in range(NSWEEP):
        padded = jnp.pad(values, ((0, 0), (1, 1), (1, 1)))
        centre = values
        values = (
            centre
            + face_up * (padded[:, :-2, 1:-1] - centre)
            + face_down * (padded[:, 2:, 1:-1] - centre)
            + face_left * (padded[:, 1:-1, :-2] - centre)
            + face_right * (padded[:, 1:-1, 2:] - centre)
        )
    return values[:, rows : 2 * rows]


def global_sum(values):
    for axis in ("col", "mem"):
        count = lax.axis_size(axis)
        stride = 1
        while stride < count:
            values = values + lax.ppermute(
                values, axis, [(i, i ^ stride) for i in range(count)]
            )
            stride *= 2
    return values


def mem_sum(values):
    parts = lax.axis_size("mem")
    pieces = values.reshape((parts, values.shape[0] // parts) + values.shape[1:])
    reduced = jnp.sum(lax.all_to_all(pieces, "mem", 0, 0, tiled=True), axis=0)
    spread = jnp.broadcast_to(reduced[None], pieces.shape)
    return lax.all_to_all(spread, "mem", 0, 0, tiled=True).reshape(values.shape)


def local_inner(first, second):
    return jnp.sum(first[0] * second[0]) + jnp.sum(first[1] * second[1])


def shards(
    perturbations,
    static_root,
    obs_jacobian,
    innovations,
    obs_weights,
    length_scale,
    obs_owner,
    obs_cell,
    obs_count,
):
    members, rows_here, columns, features = perturbations.shape
    parts = lax.axis_size("mem")
    quarter = columns // parts
    offset = lax.axis_index("mem") * quarter
    blocks = lax.axis_size("col")
    obs_dev, channels = innovations.shape
    capacity = max(2, 2 * obs_dev // blocks)
    total_slots = blocks * capacity
    coeffs = face_coefficients(length_scale)
    is_live = jnp.arange(obs_dev, dtype=jnp.int32) < obs_count[0]
    owner_ids = obs_owner[:, 0]
    onehot = (
        (owner_ids[:, None] == jnp.arange(blocks, dtype=jnp.int32)[None, :]) & is_live[:, None]
    ).astype(jnp.int32)
    slot_rank = jnp.sum((jnp.cumsum(onehot, axis=0) - onehot) * onehot, axis=1)
    slot_ids = jnp.where(is_live, owner_ids * capacity + slot_rank, total_slots)
    send_values = (
        jnp.zeros((total_slots, channels), jnp.float32).at[slot_ids].set(innovations, mode="drop")
    )
    send_cells = (
        jnp.zeros((total_slots,), jnp.float32)
        .at[slot_ids]
        .set(obs_cell.astype(jnp.float32), mode="drop")
    )
    send_marks = jnp.zeros((total_slots,), jnp.float32).at[slot_ids].set(1.0, mode="drop")
    side = jnp.zeros((blocks, 1, channels), jnp.float32)
    side = side.at[:, 0, :capacity].set(send_cells.reshape(blocks, capacity))
    side = side.at[:, 0, capacity : 2 * capacity].set(send_marks.reshape(blocks, capacity))
    packed = jnp.concatenate([send_values.reshape(blocks, capacity, channels), side], axis=1)
    got = lax.all_to_all(packed, "col", split_axis=0, concat_axis=0, tiled=True)
    got_values = got[:, :capacity, :].reshape(total_slots, channels)
    got_cells = got[:, capacity, :capacity].reshape(total_slots).astype(jnp.int32)
    got_marks = got[:, capacity, capacity : 2 * capacity].reshape(total_slots)
    obs_index = got_cells
    obs_gain = got_marks[:, None] * obs_weights[None, :]

    def spread_back(weighted):
        back = jnp.dot(weighted, obs_jacobian.T, precision=lax.Precision.HIGHEST)
        grid = jnp.zeros((rows_here * columns, features), jnp.float32).at[obs_index].add(back)
        return grid.reshape(rows_here, columns, features)

    def adjoint_map(gradient):
        own_gradient = lax.dynamic_slice_in_dim(gradient, offset, quarter, 1)
        rounded = gradient.astype(jnp.bfloat16)
        static = jnp.dot(
            own_gradient.reshape(rows_here * quarter, features),
            static_root.T,
            precision=lax.Precision.HIGHEST,
        ).reshape(rows_here, quarter, features)
        projected = jnp.einsum(
            "kyxf,yxf->kyx", perturbations, rounded, preferred_element_type=jnp.float32
        )
        return (static, sweeps(projected, coeffs))

    def forward_partial(direction):
        smoothed = sweeps(direction[1], coeffs).astype(jnp.bfloat16)
        partial_sum = jnp.einsum(
            "kyxf,kyx->yxf", perturbations, smoothed, preferred_element_type=jnp.float32
        )
        forward_static = jnp.dot(
            direction[0].reshape(rows_here * quarter, features),
            static_root,
            precision=lax.Precision.HIGHEST,
        ).reshape(rows_here, quarter, features)
        own_slice = lax.dynamic_slice_in_dim(partial_sum, offset, quarter, 1) + forward_static
        return lax.dynamic_update_slice_in_dim(partial_sum, own_slice, offset, 1)

    def hessian(direction, partial_sum):
        gathered = mem_sum(partial_sum.reshape(rows_here * columns, features)[obs_index])
        model_obs = jnp.dot(gathered, obs_jacobian, precision=lax.Precision.HIGHEST)
        adj_static, adj_ensemble = adjoint_map(spread_back(obs_gain * model_obs))
        return (direction[0] + adj_static, direction[1] + adj_ensemble)

    residual = adjoint_map(spread_back(obs_gain * got_values))
    direction = residual

    partial0 = forward_partial(direction)
    image = hessian(direction, partial0)
    sums = global_sum(
        jnp.stack(
            [
                local_inner(residual, residual),
                local_inner(direction, image),
                local_inner(image, image),
            ]
        )
    )
    norm_now, curve, image_norm = sums[0], sums[1], sums[2]
    step0 = norm_now / curve
    state = (step0 * direction[0], step0 * direction[1])
    residual = (residual[0] - step0 * image[0], residual[1] - step0 * image[1])
    norm_next = norm_now - 2.0 * step0 * curve + step0 * step0 * image_norm
    ratio = norm_next / norm_now
    direction = (residual[0] + ratio * direction[0], residual[1] + ratio * direction[1])
    norm_now = norm_next

    partial1 = forward_partial(direction)
    image = hessian(direction, partial1)
    step1 = norm_now / global_sum(local_inner(direction, image))
    state = (state[0] + step1 * direction[0], state[1] + step1 * direction[1])

    total = step0 * partial0 + step1 * partial1
    pieces = jnp.moveaxis(total.reshape(rows_here, parts, quarter, features), 1, 0)
    increment = jnp.sum(lax.all_to_all(pieces, "mem", 0, 0, tiled=True), axis=0)
    return (increment, state[0], state[1])


def solution(mesh):
    placed = (
        P("mem", "col", None, None),
        P(),
        P(),
        P("col", None),
        P(),
        P("col", None),
        P("col", None),
        P("col"),
        P("col"),
    )
    return jax.shard_map(
        shards,
        mesh=mesh,
        in_specs=placed,
        out_specs=(P("col", "mem", None), P("col", "mem", None), P("mem", "col", None)),
        check_vma=False,
    )
```

```python
import jax
import jax.numpy as jnp
from jax import lax
from jax.sharding import PartitionSpec as P

NSWEEP = 4
ITERS = 2


def neighbours(block, axis, dim, reach):
    count = lax.axis_size(axis)
    below, above = [], []
    for shift in range(1, reach + 1):
        forward = [(i, i + shift) for i in range(count - shift)]
        backward = [(target, source) for source, target in forward]
        below.insert(0, lax.ppermute(block, axis, forward))
        above.append(lax.ppermute(block, axis, backward))
    return jnp.concatenate(below + [block] + above, axis=dim)


def face_coefficients(length_scale, reach):
    rimmed = neighbours(length_scale, "col", 0, reach)
    padded = jnp.pad(rimmed, ((1, 1), (1, 1)))
    centre = padded[1:-1, 1:-1]
    return (
        jnp.sqrt(centre * padded[:-2, 1:-1]),
        jnp.sqrt(centre * padded[2:, 1:-1]),
        jnp.sqrt(centre * padded[1:-1, :-2]),
        jnp.sqrt(centre * padded[1:-1, 2:]),
    )


def sweep_steps(values, coeffs, count):
    face_up, face_down, face_left, face_right = coeffs
    for sweep_step in range(count):
        padded = jnp.pad(values, ((0, 0), (1, 1), (1, 1)))
        centre = values
        values = (
            centre
            + face_up * (padded[:, :-2, 1:-1] - centre)
            + face_down * (padded[:, 2:, 1:-1] - centre)
            + face_left * (padded[:, 1:-1, :-2] - centre)
            + face_right * (padded[:, 1:-1, 2:] - centre)
        )
    return values


def sweeps(values, coeffs):
    rows = values.shape[1]
    done = sweep_steps(neighbours(values, "col", 1, 1), coeffs, NSWEEP)
    return done[:, rows : 2 * rows]


def global_sum(values):
    axes = ("mem", "col")
    count = lax.axis_size(axes)
    spread = jnp.broadcast_to(values[None], (count,) + values.shape)
    return jnp.sum(lax.all_to_all(spread, axes, 0, 0, tiled=True), axis=0)


def mem_sum(values):
    parts = lax.axis_size("mem")
    spread = jnp.broadcast_to(values[None], (parts,) + values.shape)
    return jnp.sum(lax.all_to_all(spread, "mem", 0, 0, tiled=True), axis=0)


def local_inner(first, second):
    return jnp.sum(first[0] * second[0]) + jnp.sum(first[1] * second[1])


def shards(
    perturbations,
    static_root,
    obs_jacobian,
    innovations,
    obs_weights,
    length_scale,
    obs_owner,
    obs_cell,
    obs_count,
):
    members, rows_here, columns, features = perturbations.shape
    parts = lax.axis_size("mem")
    quarter = columns // parts
    offset = lax.axis_index("mem") * quarter
    blocks = lax.axis_size("col")
    obs_dev, channels = innovations.shape
    capacity = max(2, 2 * obs_dev // blocks)
    total_slots = blocks * capacity
    coeffs_wide = face_coefficients(length_scale, 2)
    coeffs = tuple(face[rows_here : 4 * rows_here] for face in coeffs_wide)
    is_live = jnp.arange(obs_dev, dtype=jnp.int32) < obs_count[0]
    owner_ids = obs_owner[:, 0]
    onehot = (
        (owner_ids[:, None] == jnp.arange(blocks, dtype=jnp.int32)[None, :]) & is_live[:, None]
    ).astype(jnp.int32)
    slot_rank = jnp.sum((jnp.cumsum(onehot, axis=0) - onehot) * onehot, axis=1)
    slot_ids = jnp.where(is_live, owner_ids * capacity + slot_rank, total_slots)
    source = (
        jnp.full((total_slots,), obs_dev, jnp.int32)
        .at[slot_ids]
        .set(jnp.arange(obs_dev, dtype=jnp.int32), mode="drop")
    )
    filled = source < obs_dev
    source = jnp.minimum(source, obs_dev - 1)
    send_values = jnp.where(filled[:, None], innovations[source], 0.0)
    send_cells = jnp.where(filled, obs_cell[source], 0).astype(jnp.float32)
    send_marks = filled.astype(jnp.float32)
    side = jnp.zeros((blocks, 1, channels), jnp.float32)
    side = side.at[:, 0, :capacity].set(send_cells.reshape(blocks, capacity))
    side = side.at[:, 0, capacity : 2 * capacity].set(send_marks.reshape(blocks, capacity))
    packed = jnp.concatenate([send_values.reshape(blocks, capacity, channels), side], axis=1)
    got = lax.all_to_all(packed, "col", split_axis=0, concat_axis=0, tiled=True)
    got_values = got[:, :capacity, :].reshape(total_slots, channels)
    got_cells = got[:, capacity, :capacity].reshape(total_slots).astype(jnp.int32)
    got_marks = got[:, capacity, capacity : 2 * capacity].reshape(total_slots)
    obs_index = got_cells
    obs_gain = got_marks[:, None] * obs_weights[None, :]

    def spread_back(weighted):
        back = jnp.dot(weighted, obs_jacobian.T, precision=lax.Precision.HIGHEST)
        grid = jnp.zeros((rows_here * columns, features), jnp.float32).at[obs_index].add(back)
        return grid.reshape(rows_here, columns, features)

    def adjoint_parts(gradient):
        own_gradient = lax.dynamic_slice_in_dim(gradient, offset, quarter, 1)
        rounded = gradient.astype(jnp.bfloat16)
        static = jnp.dot(
            own_gradient.reshape(rows_here * quarter, features),
            static_root.T,
            precision=lax.Precision.HIGHEST,
        ).reshape(rows_here, quarter, features)
        projected = jnp.einsum(
            "kyxf,yxf->kyx", perturbations, rounded, preferred_element_type=jnp.float32
        )
        return static, projected

    def forward_partial(static_part, smoothed_field):
        smoothed = smoothed_field.astype(jnp.bfloat16)
        partial_sum = jnp.einsum(
            "kyxf,kyx->yxf", perturbations, smoothed, preferred_element_type=jnp.float32
        )
        forward_static = jnp.dot(
            static_part.reshape(rows_here * quarter, features),
            static_root,
            precision=lax.Precision.HIGHEST,
        ).reshape(rows_here, quarter, features)
        own_slice = lax.dynamic_slice_in_dim(partial_sum, offset, quarter, 1) + forward_static
        return lax.dynamic_update_slice_in_dim(partial_sum, own_slice, offset, 1)

    def observed_gradient(partial_sum):
        gathered = mem_sum(partial_sum.reshape(rows_here * columns, features)[obs_index])
        model_obs = jnp.dot(gathered, obs_jacobian, precision=lax.Precision.HIGHEST)
        return spread_back(obs_gain * model_obs)

    right_static, right_projected = adjoint_parts(spread_back(obs_gain * got_values))
    wide = sweep_steps(neighbours(right_projected, "col", 1, 2), coeffs_wide, NSWEEP)
    right_ensemble = wide[:, 2 * rows_here : 3 * rows_here]
    wide = sweep_steps(wide, coeffs_wide, NSWEEP)
    smoothed_right = wide[:, 2 * rows_here : 3 * rows_here]
    direction = (right_static, right_ensemble)

    partial0 = forward_partial(right_static, smoothed_right)
    adj_static, adj_projected = adjoint_parts(observed_gradient(partial0))
    image = (right_static + adj_static, right_ensemble + sweeps(adj_projected, coeffs))
    sums = global_sum(
        jnp.stack(
            [
                local_inner(direction, direction),
                local_inner(direction, image),
                local_inner(image, image),
            ]
        )
    )
    smoothed_image = sweeps(image[1], coeffs)
    norm_now, curve, image_norm = sums[0], sums[1], sums[2]
    step0 = norm_now / curve
    state = (step0 * direction[0], step0 * direction[1])
    residual = (direction[0] - step0 * image[0], direction[1] - step0 * image[1])
    norm_next = norm_now - 2.0 * step0 * curve + step0 * step0 * image_norm
    ratio = norm_next / norm_now
    direction = (residual[0] + ratio * direction[0], residual[1] + ratio * direction[1])
    smoothed_direction = (smoothed_right - step0 * smoothed_image) + ratio * smoothed_right
    norm_now = norm_next

    partial1 = forward_partial(direction[0], smoothed_direction)
    adj_static, adj_projected = adjoint_parts(observed_gradient(partial1))
    curve = (
        jnp.sum(direction[0] * (direction[0] + adj_static))
        + jnp.sum(direction[1] * direction[1])
        + jnp.sum(smoothed_direction * adj_projected)
    )
    step1 = norm_now / global_sum(curve)
    state = (state[0] + step1 * direction[0], state[1] + step1 * direction[1])

    total = step0 * partial0 + step1 * partial1
    pieces = jnp.moveaxis(total.reshape(rows_here, parts, quarter, features), 1, 0)
    increment = jnp.sum(lax.all_to_all(pieces, "mem", 0, 0, tiled=True), axis=0)
    return (increment, state[0], state[1])


def solution(mesh):
    placed = (
        P("mem", "col", None, None),
        P(),
        P(),
        P("col", None),
        P(),
        P("col", None),
        P("col", None),
        P("col"),
        P("col"),
    )
    return jax.shard_map(
        shards,
        mesh=mesh,
        in_specs=placed,
        out_specs=(P("col", "mem", None), P("col", "mem", None), P("mem", "col", None)),
        check_vma=False,
    )
```

```python
import jax
import jax.numpy as jnp
from jax import lax
from jax.sharding import PartitionSpec as P

NSWEEP = 4
ITERS = 2


def neighbours(block, axis, dim, reach):
    count = lax.axis_size(axis)
    below, above = [], []
    for shift in range(1, reach + 1):
        forward = [(i, i + shift) for i in range(count - shift)]
        backward = [(target, source) for source, target in forward]
        below.insert(0, lax.ppermute(block, axis, forward))
        above.append(lax.ppermute(block, axis, backward))
    return jnp.concatenate(below + [block] + above, axis=dim)


def face_coefficients(length_scale, reach):
    rimmed = neighbours(length_scale, "col", 0, reach)
    padded = jnp.pad(rimmed, ((1, 1), (1, 1)))
    centre = padded[1:-1, 1:-1]
    return (
        jnp.sqrt(centre * padded[:-2, 1:-1]),
        jnp.sqrt(centre * padded[2:, 1:-1]),
        jnp.sqrt(centre * padded[1:-1, :-2]),
        jnp.sqrt(centre * padded[1:-1, 2:]),
    )


def sweep_steps(values, coeffs, count):
    face_up, face_down, face_left, face_right = coeffs
    for sweep_step in range(count):
        padded = jnp.pad(values, ((0, 0), (1, 1), (1, 1)))
        centre = values
        values = (
            centre
            + face_up * (padded[:, :-2, 1:-1] - centre)
            + face_down * (padded[:, 2:, 1:-1] - centre)
            + face_left * (padded[:, 1:-1, :-2] - centre)
            + face_right * (padded[:, 1:-1, 2:] - centre)
        )
    return values


def sweeps(values, coeffs):
    rows = values.shape[1]
    done = sweep_steps(neighbours(values, "col", 1, 1), coeffs, NSWEEP)
    return done[:, rows : 2 * rows]


def global_sum(values):
    axes = ("mem", "col")
    count = lax.axis_size(axes)
    spread = jnp.broadcast_to(values[None], (count,) + values.shape)
    return jnp.sum(lax.all_to_all(spread, axes, 0, 0, tiled=True), axis=0)


def local_inner(first, second):
    return jnp.sum(first[0] * second[0]) + jnp.sum(first[1] * second[1])


def shards(
    perturbations,
    static_root,
    obs_jacobian,
    innovations,
    obs_weights,
    length_scale,
    obs_owner,
    obs_cell,
    obs_count,
):
    members, rows_here, columns, features = perturbations.shape
    parts = lax.axis_size("mem")
    quarter = columns // parts
    offset = lax.axis_index("mem") * quarter
    blocks = lax.axis_size("col")
    obs_dev, channels = innovations.shape
    capacity = max(2, 2 * obs_dev // blocks)
    total_slots = blocks * capacity
    coeffs_wide = face_coefficients(length_scale, 2)
    coeffs = tuple(face[rows_here : 4 * rows_here] for face in coeffs_wide)
    is_live = jnp.arange(obs_dev, dtype=jnp.int32) < obs_count[0]
    owner_ids = obs_owner[:, 0]
    onehot = (
        (owner_ids[:, None] == jnp.arange(blocks, dtype=jnp.int32)[None, :]) & is_live[:, None]
    ).astype(jnp.int32)
    slot_rank = jnp.sum((jnp.cumsum(onehot, axis=0) - onehot) * onehot, axis=1)
    slot_ids = jnp.where(is_live, owner_ids * capacity + slot_rank, total_slots)
    source = (
        jnp.full((total_slots,), obs_dev, jnp.int32)
        .at[slot_ids]
        .set(jnp.arange(obs_dev, dtype=jnp.int32), mode="drop")
    )
    filled = source < obs_dev
    source = jnp.minimum(source, obs_dev - 1)
    send_values = jnp.where(filled[:, None], innovations[source], 0.0)
    send_cells = jnp.where(filled, obs_cell[source], 0).astype(jnp.float32)
    send_marks = filled.astype(jnp.float32)
    side = jnp.zeros((blocks, 1, channels), jnp.float32)
    side = side.at[:, 0, :capacity].set(send_cells.reshape(blocks, capacity))
    side = side.at[:, 0, capacity : 2 * capacity].set(send_marks.reshape(blocks, capacity))
    packed = jnp.concatenate([send_values.reshape(blocks, capacity, channels), side], axis=1)
    got = lax.all_to_all(packed, "col", split_axis=0, concat_axis=0, tiled=True)
    got_values = got[:, :capacity, :].reshape(total_slots, channels)
    got_cells = got[:, capacity, :capacity].reshape(total_slots).astype(jnp.int32)
    got_marks = got[:, capacity, capacity : 2 * capacity].reshape(total_slots)
    obs_index = got_cells
    obs_gain = got_marks[:, None] * obs_weights[None, :]

    def spread_back(weighted):
        back = jnp.dot(weighted, obs_jacobian.T, precision=lax.Precision.HIGHEST)
        grid = jnp.zeros((rows_here * columns, features), jnp.float32).at[obs_index].add(back)
        return grid.reshape(rows_here, columns, features)

    def adjoint_parts(gradient):
        own_gradient = lax.dynamic_slice_in_dim(gradient, offset, quarter, 1)
        rounded = gradient.astype(jnp.bfloat16)
        static = jnp.dot(
            own_gradient.reshape(rows_here * quarter, features),
            static_root.T,
            precision=lax.Precision.HIGHEST,
        ).reshape(rows_here, quarter, features)
        projected = jnp.einsum(
            "kyxf,yxf->kyx", perturbations, rounded, preferred_element_type=jnp.float32
        )
        return static, projected

    def forward_partial(static_part, smoothed_field):
        smoothed = smoothed_field.astype(jnp.bfloat16)
        partial_sum = jnp.einsum(
            "kyxf,kyx->yxf", perturbations, smoothed, preferred_element_type=jnp.float32
        )
        forward_static = jnp.dot(
            static_part.reshape(rows_here * quarter, features),
            static_root,
            precision=lax.Precision.HIGHEST,
        ).reshape(rows_here, quarter, features)
        own_slice = lax.dynamic_slice_in_dim(partial_sum, offset, quarter, 1) + forward_static
        return lax.dynamic_update_slice_in_dim(partial_sum, own_slice, offset, 1)

    def observed_gradient(partial_sum):
        gathered = partial_sum.reshape(rows_here * columns, features)[obs_index]
        pieces = jnp.moveaxis(partial_sum.reshape(rows_here, parts, quarter, features), 1, 0)
        send = jnp.concatenate(
            [
                jnp.broadcast_to(gathered[None], (parts,) + gathered.shape),
                pieces.reshape(parts, rows_here * quarter, features),
            ],
            axis=1,
        )
        got = jnp.sum(lax.all_to_all(send, "mem", 0, 0, tiled=True), axis=0)
        own_image = got[total_slots:].reshape(rows_here, quarter, features)
        model_obs = jnp.dot(got[:total_slots], obs_jacobian, precision=lax.Precision.HIGHEST)
        return spread_back(obs_gain * model_obs), own_image

    right_static, right_projected = adjoint_parts(spread_back(obs_gain * got_values))
    wide = sweep_steps(neighbours(right_projected, "col", 1, 2), coeffs_wide, NSWEEP)
    right_ensemble = wide[:, 2 * rows_here : 3 * rows_here]
    wide = sweep_steps(wide, coeffs_wide, NSWEEP)
    smoothed_right = wide[:, 2 * rows_here : 3 * rows_here]
    direction = (right_static, right_ensemble)

    partial0 = forward_partial(right_static, smoothed_right)
    gradient, own_image0 = observed_gradient(partial0)
    adj_static, adj_projected = adjoint_parts(gradient)
    image = (right_static + adj_static, right_ensemble + sweeps(adj_projected, coeffs))
    sums = global_sum(
        jnp.stack(
            [
                local_inner(direction, direction),
                local_inner(direction, image),
                local_inner(image, image),
            ]
        )
    )
    smoothed_image = sweeps(image[1], coeffs)
    norm_now, curve, image_norm = sums[0], sums[1], sums[2]
    step0 = norm_now / curve
    state = (step0 * direction[0], step0 * direction[1])
    residual = (direction[0] - step0 * image[0], direction[1] - step0 * image[1])
    norm_next = norm_now - 2.0 * step0 * curve + step0 * step0 * image_norm
    ratio = norm_next / norm_now
    direction = (residual[0] + ratio * direction[0], residual[1] + ratio * direction[1])
    smoothed_direction = (smoothed_right - step0 * smoothed_image) + ratio * smoothed_right
    norm_now = norm_next

    partial1 = forward_partial(direction[0], smoothed_direction)
    gradient, own_image1 = observed_gradient(partial1)
    adj_static, adj_projected = adjoint_parts(gradient)
    curve = (
        jnp.sum(direction[0] * (direction[0] + adj_static))
        + jnp.sum(direction[1] * direction[1])
        + jnp.sum(smoothed_direction * adj_projected)
    )
    step1 = norm_now / global_sum(curve)
    state = (state[0] + step1 * direction[0], state[1] + step1 * direction[1])

    increment = step0 * own_image0 + step1 * own_image1
    return (increment, state[0], state[1])


def solution(mesh):
    placed = (
        P("mem", "col", None, None),
        P(),
        P(),
        P("col", None),
        P(),
        P("col", None),
        P("col", None),
        P("col"),
        P("col"),
    )
    return jax.shard_map(
        shards,
        mesh=mesh,
        in_specs=placed,
        out_specs=(P("col", "mem", None), P("col", "mem", None), P("mem", "col", None)),
        check_vma=False,
    )
```

```python
import jax
import jax.numpy as jnp
from jax import lax
from jax.sharding import PartitionSpec as P

NSWEEP = 4
ITERS = 2


def neighbours(block, axis, dim, reach):
    count = lax.axis_size(axis)
    below, above = [], []
    for shift in range(1, reach + 1):
        forward = [(i, i + shift) for i in range(count - shift)]
        backward = [(target, source) for source, target in forward]
        below.insert(0, lax.ppermute(block, axis, forward))
        above.append(lax.ppermute(block, axis, backward))
    return jnp.concatenate(below + [block] + above, axis=dim)


def face_coefficients(length_scale, reach):
    rimmed = neighbours(length_scale, "col", 0, reach)
    padded = jnp.pad(rimmed, ((1, 1), (1, 1)))
    centre = padded[1:-1, 1:-1]
    return (
        jnp.sqrt(centre * padded[:-2, 1:-1]),
        jnp.sqrt(centre * padded[2:, 1:-1]),
        jnp.sqrt(centre * padded[1:-1, :-2]),
        jnp.sqrt(centre * padded[1:-1, 2:]),
    )


def sweep_steps(values, coeffs, count):
    face_up, face_down, face_left, face_right = coeffs
    for sweep_step in range(count):
        padded = jnp.pad(values, ((0, 0), (1, 1), (1, 1)))
        centre = values
        values = (
            centre
            + face_up * (padded[:, :-2, 1:-1] - centre)
            + face_down * (padded[:, 2:, 1:-1] - centre)
            + face_left * (padded[:, 1:-1, :-2] - centre)
            + face_right * (padded[:, 1:-1, 2:] - centre)
        )
    return values


def sweeps(values, coeffs):
    rows = values.shape[1]
    done = sweep_steps(neighbours(values, "col", 1, 1), coeffs, NSWEEP)
    return done[:, rows : 2 * rows]


def global_sum(values):
    axes = ("mem", "col")
    count = lax.axis_size(axes)
    spread = jnp.broadcast_to(values[None], (count,) + values.shape)
    return jnp.sum(lax.all_to_all(spread, axes, 0, 0, tiled=True), axis=0)


def local_inner(first, second):
    return jnp.sum(first[0] * second[0]) + jnp.sum(first[1] * second[1])


def shards(
    perturbations,
    static_root,
    obs_jacobian,
    innovations,
    obs_weights,
    length_scale,
    obs_owner,
    obs_cell,
    obs_count,
):
    members, rows_here, columns, features = perturbations.shape
    parts = lax.axis_size("mem")
    quarter = columns // parts
    offset = lax.axis_index("mem") * quarter
    blocks = lax.axis_size("col")
    obs_dev, channels = innovations.shape
    capacity = max(2, 2 * obs_dev // blocks)
    total_slots = blocks * capacity
    coeffs_wide = face_coefficients(length_scale, 2)
    coeffs = tuple(face[rows_here : 4 * rows_here] for face in coeffs_wide)
    is_live = jnp.arange(obs_dev, dtype=jnp.int32) < obs_count[0]
    owner_ids = obs_owner[:, 0]
    onehot = (
        (owner_ids[:, None] == jnp.arange(blocks, dtype=jnp.int32)[None, :]) & is_live[:, None]
    ).astype(jnp.int32)
    slot_rank = jnp.sum((jnp.cumsum(onehot, axis=0) - onehot) * onehot, axis=1)
    slot_ids = jnp.where(is_live, owner_ids * capacity + slot_rank, total_slots)
    source = (
        jnp.full((total_slots,), obs_dev, jnp.int32)
        .at[slot_ids]
        .set(jnp.arange(obs_dev, dtype=jnp.int32), mode="drop")
    )
    filled = source < obs_dev
    source = jnp.minimum(source, obs_dev - 1)
    send_values = jnp.where(filled[:, None], innovations[source], 0.0)
    send_cells = jnp.where(filled, obs_cell[source], 0).astype(jnp.float32)
    send_marks = filled.astype(jnp.float32)
    side = jnp.zeros((blocks, 1, channels), jnp.float32)
    side = side.at[:, 0, :capacity].set(send_cells.reshape(blocks, capacity))
    side = side.at[:, 0, capacity : 2 * capacity].set(send_marks.reshape(blocks, capacity))
    packed = jnp.concatenate([send_values.reshape(blocks, capacity, channels), side], axis=1)
    got = lax.all_to_all(packed, "col", split_axis=0, concat_axis=0, tiled=True)
    got_values = got[:, :capacity, :].reshape(total_slots, channels)
    got_cells = got[:, capacity, :capacity].reshape(total_slots).astype(jnp.int32)
    got_marks = got[:, capacity, capacity : 2 * capacity].reshape(total_slots)
    obs_index = got_cells
    obs_gain = got_marks[:, None] * obs_weights[None, :]

    def spread_back(weighted):
        back = jnp.dot(weighted, obs_jacobian.T, precision=lax.Precision.HIGHEST)
        grid = jnp.zeros((rows_here * columns, features), jnp.float32).at[obs_index].add(back)
        return grid.reshape(rows_here, columns, features)

    def adjoint_parts(gradient):
        own_gradient = lax.dynamic_slice_in_dim(gradient, offset, quarter, 1)
        rounded = gradient.astype(jnp.bfloat16)
        static = jnp.dot(
            own_gradient.reshape(rows_here * quarter, features),
            static_root.T,
            precision=lax.Precision.HIGHEST,
        ).reshape(rows_here, quarter, features)
        projected = jnp.einsum(
            "kyxf,yxf->kyx", perturbations, rounded, preferred_element_type=jnp.float32
        )
        return static, projected

    def forward_partial(static_part, smoothed_field):
        smoothed = smoothed_field.astype(jnp.bfloat16)
        partial_sum = jnp.einsum(
            "kyxf,kyx->yxf", perturbations, smoothed, preferred_element_type=jnp.float32
        )
        forward_static = jnp.dot(
            static_part.reshape(rows_here * quarter, features),
            static_root,
            precision=lax.Precision.HIGHEST,
        ).reshape(rows_here, quarter, features)
        own_slice = lax.dynamic_slice_in_dim(partial_sum, offset, quarter, 1) + forward_static
        return lax.dynamic_update_slice_in_dim(partial_sum, own_slice, offset, 1)

    cell_x = obs_index % columns
    in_quarter = (cell_x >= offset) & (cell_x < offset + quarter)
    quarter_index = jnp.where(in_quarter, (obs_index // columns) * quarter + cell_x - offset, 0)
    quarter_gain = jnp.where(in_quarter[:, None], obs_gain, 0.0)

    def observed_adjoint(partial_sum):
        pieces = jnp.moveaxis(partial_sum.reshape(rows_here, parts, quarter, features), 1, 0)
        own_image = jnp.sum(lax.all_to_all(pieces, "mem", 0, 0, tiled=True), axis=0)
        gathered = own_image.reshape(rows_here * quarter, features)[quarter_index]
        model_obs = jnp.dot(gathered, obs_jacobian, precision=lax.Precision.HIGHEST)
        back = jnp.dot(quarter_gain * model_obs, obs_jacobian.T, precision=lax.Precision.HIGHEST)
        own_gradient = jnp.zeros((rows_here * quarter, features), jnp.float32).at[quarter_index].add(back)
        static = jnp.dot(own_gradient, static_root.T, precision=lax.Precision.HIGHEST).reshape(
            rows_here, quarter, features
        )
        rounded = own_gradient.reshape(rows_here, quarter, features).astype(jnp.bfloat16)
        spread = jnp.broadcast_to(rounded[None], (parts,) + rounded.shape)
        quarters = lax.all_to_all(spread, "mem", 0, 0, tiled=True)
        rounded = jnp.moveaxis(quarters, 0, 1).reshape(rows_here, columns, features)
        projected = jnp.einsum(
            "kyxf,yxf->kyx", perturbations, rounded, preferred_element_type=jnp.float32
        )
        return own_image, static, projected

    right_static, right_projected = adjoint_parts(spread_back(obs_gain * got_values))
    wide = sweep_steps(neighbours(right_projected, "col", 1, 2), coeffs_wide, NSWEEP)
    right_ensemble = wide[:, 2 * rows_here : 3 * rows_here]
    wide = sweep_steps(wide, coeffs_wide, NSWEEP)
    smoothed_right = wide[:, 2 * rows_here : 3 * rows_here]
    direction = (right_static, right_ensemble)

    partial0 = forward_partial(right_static, smoothed_right)
    own_image0, adj_static, adj_projected = observed_adjoint(partial0)
    image = (right_static + adj_static, right_ensemble + sweeps(adj_projected, coeffs))
    sums = global_sum(
        jnp.stack(
            [
                local_inner(direction, direction),
                local_inner(direction, image),
                local_inner(image, image),
            ]
        )
    )
    smoothed_image = sweeps(image[1], coeffs)
    norm_now, curve, image_norm = sums[0], sums[1], sums[2]
    step0 = norm_now / curve
    state = (step0 * direction[0], step0 * direction[1])
    residual = (direction[0] - step0 * image[0], direction[1] - step0 * image[1])
    norm_next = norm_now - 2.0 * step0 * curve + step0 * step0 * image_norm
    ratio = norm_next / norm_now
    direction = (residual[0] + ratio * direction[0], residual[1] + ratio * direction[1])
    smoothed_direction = (smoothed_right - step0 * smoothed_image) + ratio * smoothed_right
    norm_now = norm_next

    partial1 = forward_partial(direction[0], smoothed_direction)
    own_image1, adj_static, adj_projected = observed_adjoint(partial1)
    curve = (
        jnp.sum(direction[0] * (direction[0] + adj_static))
        + jnp.sum(direction[1] * direction[1])
        + jnp.sum(smoothed_direction * adj_projected)
    )
    step1 = norm_now / global_sum(curve)
    state = (state[0] + step1 * direction[0], state[1] + step1 * direction[1])

    increment = step0 * own_image0 + step1 * own_image1
    return (increment, state[0], state[1])


def solution(mesh):
    placed = (
        P("mem", "col", None, None),
        P(),
        P(),
        P("col", None),
        P(),
        P("col", None),
        P("col", None),
        P("col"),
        P("col"),
    )
    return jax.shard_map(
        shards,
        mesh=mesh,
        in_specs=placed,
        out_specs=(P("col", "mem", None), P("col", "mem", None), P("mem", "col", None)),
        check_vma=False,
    )
```

```python
import jax
import jax.numpy as jnp
from jax import lax
from jax.sharding import PartitionSpec as P

NSWEEP = 4
ITERS = 2


def neighbours(block, axis, dim, reach):
    count = lax.axis_size(axis)
    below, above = [], []
    for shift in range(1, reach + 1):
        forward = [(i, i + shift) for i in range(count - shift)]
        backward = [(target, source) for source, target in forward]
        below.insert(0, lax.ppermute(block, axis, forward))
        above.append(lax.ppermute(block, axis, backward))
    return jnp.concatenate(below + [block] + above, axis=dim)


def face_coefficients(length_scale, reach):
    rimmed = neighbours(length_scale, "col", 0, reach)
    padded = jnp.pad(rimmed, ((1, 1), (1, 1)))
    centre = padded[1:-1, 1:-1]
    return (
        jnp.sqrt(centre * padded[:-2, 1:-1]),
        jnp.sqrt(centre * padded[2:, 1:-1]),
        jnp.sqrt(centre * padded[1:-1, :-2]),
        jnp.sqrt(centre * padded[1:-1, 2:]),
    )


def sweep_steps(values, coeffs, count):
    face_up, face_down, face_left, face_right = coeffs
    for sweep_step in range(count):
        padded = jnp.pad(values, ((0, 0), (1, 1), (1, 1)))
        centre = values
        values = (
            centre
            + face_up * (padded[:, :-2, 1:-1] - centre)
            + face_down * (padded[:, 2:, 1:-1] - centre)
            + face_left * (padded[:, 1:-1, :-2] - centre)
            + face_right * (padded[:, 1:-1, 2:] - centre)
        )
    return values


def sweeps(values, coeffs):
    rows = values.shape[1]
    done = sweep_steps(neighbours(values, "col", 1, 1), coeffs, NSWEEP)
    return done[:, rows : 2 * rows]


def global_sum(values):
    axes = ("mem", "col")
    count = lax.axis_size(axes)
    spread = jnp.broadcast_to(values[None], (count,) + values.shape)
    return jnp.sum(lax.all_to_all(spread, axes, 0, 0, tiled=True), axis=0)


def local_inner(first, second):
    return jnp.sum(first[0] * second[0]) + jnp.sum(first[1] * second[1])


def shards(
    perturbations,
    static_root,
    obs_jacobian,
    innovations,
    obs_weights,
    length_scale,
    obs_owner,
    obs_cell,
    obs_count,
):
    members, rows_here, columns, features = perturbations.shape
    parts = lax.axis_size("mem")
    quarter = columns // parts
    offset = lax.axis_index("mem") * quarter
    blocks = lax.axis_size("col")
    obs_dev, channels = innovations.shape
    capacity = max(2, 2 * obs_dev // blocks)
    total_slots = blocks * capacity
    coeffs_wide = face_coefficients(length_scale, 2)
    coeffs = tuple(face[rows_here : 4 * rows_here] for face in coeffs_wide)
    is_live = jnp.arange(obs_dev, dtype=jnp.int32) < obs_count[0]
    owner_ids = obs_owner[:, 0]
    onehot = (
        (owner_ids[:, None] == jnp.arange(blocks, dtype=jnp.int32)[None, :]) & is_live[:, None]
    ).astype(jnp.int32)
    slot_rank = jnp.sum((jnp.cumsum(onehot, axis=0) - onehot) * onehot, axis=1)
    slot_ids = jnp.where(is_live, owner_ids * capacity + slot_rank, total_slots)
    source = (
        jnp.full((total_slots,), obs_dev, jnp.int32)
        .at[slot_ids]
        .set(jnp.arange(obs_dev, dtype=jnp.int32), mode="drop")
    )
    filled = source < obs_dev
    source = jnp.minimum(source, obs_dev - 1)
    send_values = jnp.where(filled[:, None], innovations[source], 0.0)
    send_cells = jnp.where(filled, obs_cell[source], 0).astype(jnp.float32)
    send_marks = filled.astype(jnp.float32)
    side = jnp.concatenate(
        [
            send_cells.reshape(blocks, capacity),
            send_marks.reshape(blocks, capacity),
            jnp.zeros((blocks, channels - 2 * capacity), jnp.float32),
        ],
        axis=1,
    )[:, None, :]
    packed = jnp.concatenate([send_values.reshape(blocks, capacity, channels), side], axis=1)
    got = lax.all_to_all(packed, "col", split_axis=0, concat_axis=0, tiled=True)
    got_values = got[:, :capacity, :].reshape(total_slots, channels)
    got_cells = got[:, capacity, :capacity].reshape(total_slots).astype(jnp.int32)
    got_marks = got[:, capacity, capacity : 2 * capacity].reshape(total_slots)
    obs_index = got_cells
    obs_gain = got_marks[:, None] * obs_weights[None, :]

    def spread_back(weighted):
        back = jnp.dot(weighted, obs_jacobian.T, precision=lax.Precision.HIGHEST)
        grid = jnp.zeros((rows_here * columns, features), jnp.float32).at[obs_index].add(back)
        return grid.reshape(rows_here, columns, features)

    def adjoint_parts(gradient):
        own_gradient = lax.dynamic_slice_in_dim(gradient, offset, quarter, 1)
        rounded = gradient.astype(jnp.bfloat16)
        static = jnp.dot(
            own_gradient.reshape(rows_here * quarter, features),
            static_root.T,
            precision=lax.Precision.HIGHEST,
        ).reshape(rows_here, quarter, features)
        projected = jnp.einsum(
            "kyxf,yxf->kyx", perturbations, rounded, preferred_element_type=jnp.float32
        )
        return static, projected

    def forward_partial(static_part, smoothed_field):
        smoothed = smoothed_field.astype(jnp.bfloat16)
        partial_sum = jnp.einsum(
            "kyxf,kyx->yxf", perturbations, smoothed, preferred_element_type=jnp.float32
        )
        forward_static = jnp.dot(
            static_part.reshape(rows_here * quarter, features),
            static_root,
            precision=lax.Precision.HIGHEST,
        ).reshape(rows_here, quarter, features)
        own_slice = lax.dynamic_slice_in_dim(partial_sum, offset, quarter, 1) + forward_static
        return lax.dynamic_update_slice_in_dim(partial_sum, own_slice, offset, 1)

    cell_x = obs_index % columns
    in_quarter = (cell_x >= offset) & (cell_x < offset + quarter)
    quarter_index = jnp.where(in_quarter, (obs_index // columns) * quarter + cell_x - offset, 0)
    quarter_gain = jnp.where(in_quarter[:, None], obs_gain, 0.0)

    def observed(partial_sum):
        pieces = jnp.moveaxis(partial_sum.reshape(rows_here, parts, quarter, features), 1, 0)
        own_image = jnp.sum(lax.all_to_all(pieces, "mem", 0, 0, tiled=True), axis=0)
        gathered = own_image.reshape(rows_here * quarter, features)[quarter_index]
        model_obs = jnp.dot(gathered, obs_jacobian, precision=lax.Precision.HIGHEST)
        return own_image, model_obs

    def observed_adjoint(model_obs):
        back = jnp.dot(quarter_gain * model_obs, obs_jacobian.T, precision=lax.Precision.HIGHEST)
        own_gradient = jnp.zeros((rows_here * quarter, features), jnp.float32).at[quarter_index].add(back)
        static = jnp.dot(own_gradient, static_root.T, precision=lax.Precision.HIGHEST).reshape(
            rows_here, quarter, features
        )
        rounded = own_gradient.reshape(rows_here, quarter, features).astype(jnp.bfloat16)
        spread = jnp.broadcast_to(rounded[None], (parts,) + rounded.shape)
        quarters = lax.all_to_all(spread, "mem", 0, 0, tiled=True)
        rounded = jnp.moveaxis(quarters, 0, 1).reshape(rows_here, columns, features)
        projected = jnp.einsum(
            "kyxf,yxf->kyx", perturbations, rounded, preferred_element_type=jnp.float32
        )
        return static, projected

    right_static, right_projected = adjoint_parts(spread_back(obs_gain * got_values))
    wide = sweep_steps(neighbours(right_projected, "col", 1, 2), coeffs_wide, NSWEEP)
    right_ensemble = wide[:, 2 * rows_here : 3 * rows_here]
    wide = sweep_steps(wide, coeffs_wide, NSWEEP)
    smoothed_right = wide[:, 2 * rows_here : 3 * rows_here]
    direction = (right_static, right_ensemble)

    partial0 = forward_partial(right_static, smoothed_right)
    own_image0, model_obs = observed(partial0)
    adj_static, adj_projected = observed_adjoint(model_obs)
    image = (right_static + adj_static, right_ensemble + sweeps(adj_projected, coeffs))
    sums = global_sum(
        jnp.stack(
            [
                local_inner(direction, direction),
                local_inner(direction, image),
                local_inner(image, image),
            ]
        )
    )
    smoothed_image = sweeps(image[1], coeffs)
    norm_now, curve, image_norm = sums[0], sums[1], sums[2]
    step0 = norm_now / curve
    state = (step0 * direction[0], step0 * direction[1])
    residual = (direction[0] - step0 * image[0], direction[1] - step0 * image[1])
    norm_next = norm_now - 2.0 * step0 * curve + step0 * step0 * image_norm
    ratio = norm_next / norm_now
    direction = (residual[0] + ratio * direction[0], residual[1] + ratio * direction[1])
    smoothed_direction = (smoothed_right - step0 * smoothed_image) + ratio * smoothed_right
    norm_now = norm_next

    partial1 = forward_partial(direction[0], smoothed_direction)
    own_image1, model_obs = observed(partial1)
    curve = (
        jnp.sum(direction[0] * direction[0])
        + jnp.sum(direction[1] * direction[1])
        + jnp.sum(quarter_gain * model_obs * model_obs)
    )
    step1 = norm_now / global_sum(curve)
    state = (state[0] + step1 * direction[0], state[1] + step1 * direction[1])

    increment = step0 * own_image0 + step1 * own_image1
    return (increment, state[0], state[1])


def solution(mesh):
    placed = (
        P("mem", "col", None, None),
        P(),
        P(),
        P("col", None),
        P(),
        P("col", None),
        P("col", None),
        P("col"),
        P("col"),
    )
    return jax.shard_map(
        shards,
        mesh=mesh,
        in_specs=placed,
        out_specs=(P("col", "mem", None), P("col", "mem", None), P("mem", "col", None)),
        check_vma=False,
    )
```

```python
import jax
import jax.numpy as jnp
from jax import lax
from jax.sharding import PartitionSpec as P

NSWEEP = 4
ITERS = 2


def neighbours(block, axis, dim, reach):
    count = lax.axis_size(axis)
    below, above = [], []
    for shift in range(1, reach + 1):
        forward = [(i, i + shift) for i in range(count - shift)]
        backward = [(target, source) for source, target in forward]
        below.insert(0, lax.ppermute(block, axis, forward))
        above.append(lax.ppermute(block, axis, backward))
    return jnp.concatenate(below + [block] + above, axis=dim)


def face_coefficients(length_scale, reach):
    rimmed = neighbours(length_scale, "col", 0, reach)
    padded = jnp.pad(rimmed, ((1, 1), (1, 1)))
    centre = padded[1:-1, 1:-1]
    return (
        jnp.sqrt(centre * padded[:-2, 1:-1]),
        jnp.sqrt(centre * padded[2:, 1:-1]),
        jnp.sqrt(centre * padded[1:-1, :-2]),
        jnp.sqrt(centre * padded[1:-1, 2:]),
    )


def sweep_steps(values, coeffs, count):
    face_up, face_down, face_left, face_right = coeffs
    for sweep_step in range(count):
        padded = jnp.pad(values, ((0, 0), (1, 1), (1, 1)))
        centre = values
        values = (
            centre
            + face_up * (padded[:, :-2, 1:-1] - centre)
            + face_down * (padded[:, 2:, 1:-1] - centre)
            + face_left * (padded[:, 1:-1, :-2] - centre)
            + face_right * (padded[:, 1:-1, 2:] - centre)
        )
    return values


def sweeps(values, coeffs):
    rows = values.shape[1]
    done = sweep_steps(neighbours(values, "col", 1, 1), coeffs, NSWEEP)
    return done[:, rows : 2 * rows]


def global_sum(values):
    axes = ("mem", "col")
    count = lax.axis_size(axes)
    spread = jnp.broadcast_to(values[None], (count,) + values.shape)
    return jnp.sum(lax.all_to_all(spread, axes, 0, 0, tiled=True), axis=0)


def local_inner(first, second):
    return jnp.sum(first[0] * second[0]) + jnp.sum(first[1] * second[1])


def shards(
    perturbations,
    static_root,
    obs_jacobian,
    innovations,
    obs_weights,
    length_scale,
    obs_owner,
    obs_cell,
    obs_count,
):
    members, rows_here, columns, features = perturbations.shape
    parts = lax.axis_size("mem")
    quarter = columns // parts
    offset = lax.axis_index("mem") * quarter
    blocks = lax.axis_size("col")
    obs_dev, channels = innovations.shape
    capacity = max(2, 2 * obs_dev // blocks)
    total_slots = blocks * capacity
    coeffs_wide = face_coefficients(length_scale, 2)
    coeffs = tuple(face[rows_here : 4 * rows_here] for face in coeffs_wide)
    is_live = jnp.arange(obs_dev, dtype=jnp.int32) < obs_count[0]
    owner_ids = obs_owner[:, 0]
    onehot = (
        (owner_ids[:, None] == jnp.arange(blocks, dtype=jnp.int32)[None, :]) & is_live[:, None]
    ).astype(jnp.int32)
    slot_rank = jnp.sum((jnp.cumsum(onehot, axis=0) - onehot) * onehot, axis=1)
    slot_ids = jnp.where(is_live, owner_ids * capacity + slot_rank, total_slots)
    source = (
        jnp.full((total_slots,), obs_dev, jnp.int32)
        .at[slot_ids]
        .set(jnp.arange(obs_dev, dtype=jnp.int32), mode="drop")
    )
    filled = source < obs_dev
    source = jnp.minimum(source, obs_dev - 1)
    send_values = jnp.where(filled[:, None], innovations[source], 0.0)
    send_cells = jnp.where(filled, obs_cell[source], 0).astype(jnp.float32)
    send_marks = filled.astype(jnp.float32)
    side = jnp.concatenate(
        [
            send_cells.reshape(blocks, capacity),
            send_marks.reshape(blocks, capacity),
            jnp.zeros((blocks, channels - 2 * capacity), jnp.float32),
        ],
        axis=1,
    )[:, None, :]
    packed = jnp.concatenate([send_values.reshape(blocks, capacity, channels), side], axis=1)
    got = lax.all_to_all(packed, "col", split_axis=0, concat_axis=0, tiled=True)
    got_values = got[:, :capacity, :].reshape(total_slots, channels)
    got_cells = got[:, capacity, :capacity].reshape(total_slots).astype(jnp.int32)
    got_marks = got[:, capacity, capacity : 2 * capacity].reshape(total_slots)
    obs_index = got_cells
    obs_gain = got_marks[:, None] * obs_weights[None, :]

    def spread_back(weighted):
        back = jnp.dot(weighted, obs_jacobian.T, precision=lax.Precision.HIGHEST)
        grid = jnp.zeros((rows_here * columns, features), jnp.float32).at[obs_index].add(back)
        return grid.reshape(rows_here, columns, features)

    def adjoint_parts(gradient):
        own_gradient = lax.dynamic_slice_in_dim(gradient, offset, quarter, 1)
        rounded = gradient.astype(jnp.bfloat16)
        static = jnp.dot(
            own_gradient.reshape(rows_here * quarter, features),
            static_root.T,
            precision=lax.Precision.HIGHEST,
        ).reshape(rows_here, quarter, features)
        projected = jnp.einsum(
            "kyxf,yxf->kyx", perturbations, rounded, preferred_element_type=jnp.float32
        )
        return static, projected

    def forward_partial(static_part, smoothed_field):
        smoothed = smoothed_field.astype(jnp.bfloat16)
        partial_sum = jnp.einsum(
            "kyxf,kyx->yxf", perturbations, smoothed, preferred_element_type=jnp.float32
        )
        forward_static = jnp.dot(
            static_part.reshape(rows_here * quarter, features),
            static_root,
            precision=lax.Precision.HIGHEST,
        ).reshape(rows_here, quarter, features)
        own_slice = lax.dynamic_slice_in_dim(partial_sum, offset, quarter, 1) + forward_static
        return lax.dynamic_update_slice_in_dim(partial_sum, own_slice, offset, 1)

    cell_x = obs_index % columns
    in_quarter = (cell_x >= offset) & (cell_x < offset + quarter)
    quarter_index = jnp.where(in_quarter, (obs_index // columns) * quarter + cell_x - offset, 0)
    quarter_gain = jnp.where(in_quarter[:, None], obs_gain, 0.0)

    def observed(partial_sum):
        pieces = jnp.moveaxis(partial_sum.reshape(rows_here, parts, quarter, features), 1, 0)
        own_image = jnp.sum(lax.all_to_all(pieces, "mem", 0, 0, tiled=True), axis=0)
        gathered = own_image.reshape(rows_here * quarter, features)[quarter_index]
        model_obs = jnp.dot(gathered, obs_jacobian, precision=lax.Precision.HIGHEST)
        return own_image, model_obs

    def observed_adjoint(model_obs):
        back = jnp.dot(quarter_gain * model_obs, obs_jacobian.T, precision=lax.Precision.HIGHEST)
        own_gradient = jnp.zeros((rows_here * quarter, features), jnp.float32).at[quarter_index].add(back)
        static = jnp.dot(own_gradient, static_root.T, precision=lax.Precision.HIGHEST).reshape(
            rows_here, quarter, features
        )
        rounded = own_gradient.reshape(rows_here, quarter, features).astype(jnp.bfloat16)
        spread = jnp.broadcast_to(rounded[None], (parts,) + rounded.shape)
        quarters = lax.all_to_all(spread, "mem", 0, 0, tiled=True)
        rounded = jnp.moveaxis(quarters, 0, 1).reshape(rows_here, columns, features)
        projected = jnp.einsum(
            "kyxf,yxf->kyx", perturbations, rounded, preferred_element_type=jnp.float32
        )
        return static, projected

    right_static, right_projected = adjoint_parts(spread_back(obs_gain * got_values))
    wide = sweep_steps(neighbours(right_projected, "col", 1, 2), coeffs_wide, NSWEEP)
    right_ensemble = wide[:, 2 * rows_here : 3 * rows_here]
    wide = sweep_steps(wide, coeffs_wide, NSWEEP)
    smoothed_right = wide[:, 2 * rows_here : 3 * rows_here]
    direction = (right_static, right_ensemble)

    partial0 = forward_partial(right_static, smoothed_right)
    own_image0, model_obs = observed(partial0)
    adj_static, adj_projected = observed_adjoint(model_obs)
    image = (right_static + adj_static, right_ensemble + sweeps(adj_projected, coeffs))
    sums = global_sum(
        jnp.stack(
            [
                local_inner(direction, direction),
                local_inner(direction, image),
                local_inner(image, image),
            ]
        )
    )
    smoothed_image = sweeps(image[1], coeffs)
    ensemble_parts = jnp.stack(
        [
            jnp.einsum(
                "kyxf,kyx->yxf", perturbations, field, preferred_element_type=jnp.float32
            )
            for field in (smoothed_right, smoothed_image)
        ]
    )
    pieces = jnp.moveaxis(
        ensemble_parts.reshape(2, rows_here, parts, quarter, features), 2, 0
    )
    own_right, own_image = jnp.sum(lax.all_to_all(pieces, "mem", 0, 0, tiled=True), axis=0)
    norm_now, curve, image_norm = sums[0], sums[1], sums[2]
    step0 = norm_now / curve
    state = (step0 * direction[0], step0 * direction[1])
    residual = (direction[0] - step0 * image[0], direction[1] - step0 * image[1])
    norm_next = norm_now - 2.0 * step0 * curve + step0 * step0 * image_norm
    ratio = norm_next / norm_now
    direction = (residual[0] + ratio * direction[0], residual[1] + ratio * direction[1])
    norm_now = norm_next

    forward_static = jnp.dot(
        direction[0].reshape(rows_here * quarter, features),
        static_root,
        precision=lax.Precision.HIGHEST,
    ).reshape(rows_here, quarter, features)
    own_image1 = ((own_right - step0 * own_image) + ratio * own_right) + forward_static
    gathered = own_image1.reshape(rows_here * quarter, features)[quarter_index]
    model_obs = jnp.dot(gathered, obs_jacobian, precision=lax.Precision.HIGHEST)
    curve = (
        jnp.sum(direction[0] * direction[0])
        + jnp.sum(direction[1] * direction[1])
        + jnp.sum(quarter_gain * model_obs * model_obs)
    )
    step1 = norm_now / global_sum(curve)
    state = (state[0] + step1 * direction[0], state[1] + step1 * direction[1])

    increment = step0 * own_image0 + step1 * own_image1
    return (increment, state[0], state[1])


def solution(mesh):
    placed = (
        P("mem", "col", None, None),
        P(),
        P(),
        P("col", None),
        P(),
        P("col", None),
        P("col", None),
        P("col"),
        P("col"),
    )
    return jax.shard_map(
        shards,
        mesh=mesh,
        in_specs=placed,
        out_specs=(P("col", "mem", None), P("col", "mem", None), P("mem", "col", None)),
        check_vma=False,
    )
```

```python
import jax
import jax.numpy as jnp
from jax import lax
from jax.sharding import PartitionSpec as P

NSWEEP = 4
ITERS = 2


def neighbours(block, axis, dim, reach):
    count = lax.axis_size(axis)
    below, above = [], []
    for shift in range(1, reach + 1):
        forward = [(i, i + shift) for i in range(count - shift)]
        backward = [(target, source) for source, target in forward]
        below.insert(0, lax.ppermute(block, axis, forward))
        above.append(lax.ppermute(block, axis, backward))
    return jnp.concatenate(below + [block] + above, axis=dim)


def face_coefficients(length_scale, reach):
    rimmed = neighbours(length_scale, "col", 0, reach)
    padded = jnp.pad(rimmed, ((1, 1), (1, 1)))
    centre = padded[1:-1, 1:-1]
    return (
        jnp.sqrt(centre * padded[:-2, 1:-1]),
        jnp.sqrt(centre * padded[2:, 1:-1]),
        jnp.sqrt(centre * padded[1:-1, :-2]),
        jnp.sqrt(centre * padded[1:-1, 2:]),
    )


def sweep_steps(values, coeffs, count):
    face_up, face_down, face_left, face_right = coeffs
    for sweep_step in range(count):
        padded = jnp.pad(values, ((0, 0), (1, 1), (1, 1)))
        centre = values
        values = (
            centre
            + face_up * (padded[:, :-2, 1:-1] - centre)
            + face_down * (padded[:, 2:, 1:-1] - centre)
            + face_left * (padded[:, 1:-1, :-2] - centre)
            + face_right * (padded[:, 1:-1, 2:] - centre)
        )
    return values


def sweeps(values, coeffs):
    rows = values.shape[1]
    done = sweep_steps(neighbours(values, "col", 1, 1), coeffs, NSWEEP)
    return done[:, rows : 2 * rows]


def global_sum(values):
    axes = ("mem", "col")
    count = lax.axis_size(axes)
    spread = jnp.broadcast_to(values[None], (count,) + values.shape)
    return jnp.sum(lax.all_to_all(spread, axes, 0, 0, tiled=True), axis=0)


def local_inner(first, second):
    return jnp.sum(first[0] * second[0]) + jnp.sum(first[1] * second[1])


def shards(
    perturbations,
    static_root,
    obs_jacobian,
    innovations,
    obs_weights,
    length_scale,
    obs_owner,
    obs_cell,
    obs_count,
):
    members, rows_here, columns, features = perturbations.shape
    parts = lax.axis_size("mem")
    quarter = columns // parts
    offset = lax.axis_index("mem") * quarter
    blocks = lax.axis_size("col")
    obs_dev, channels = innovations.shape
    capacity = max(2, 2 * obs_dev // blocks)
    total_slots = blocks * capacity
    coeffs_wide = face_coefficients(length_scale, 2)
    coeffs = tuple(face[rows_here : 4 * rows_here] for face in coeffs_wide)
    is_live = jnp.arange(obs_dev, dtype=jnp.int32) < obs_count[0]
    owner_ids = obs_owner[:, 0]
    onehot = (
        (owner_ids[:, None] == jnp.arange(blocks, dtype=jnp.int32)[None, :]) & is_live[:, None]
    ).astype(jnp.int32)
    slot_rank = jnp.sum((jnp.cumsum(onehot, axis=0) - onehot) * onehot, axis=1)
    slot_ids = jnp.where(is_live, owner_ids * capacity + slot_rank, total_slots)
    send_values = (
        jnp.zeros((total_slots, channels), jnp.float32).at[slot_ids].set(innovations, mode="drop")
    )
    tags = jnp.stack([obs_cell.astype(jnp.float32), jnp.ones((obs_dev,), jnp.float32)], axis=1)
    tags = jnp.zeros((total_slots, 2), jnp.float32).at[slot_ids].set(tags, mode="drop")
    side = jnp.concatenate(
        [
            jnp.swapaxes(tags.reshape(blocks, capacity, 2), 1, 2).reshape(blocks, 2 * capacity),
            jnp.zeros((blocks, channels - 2 * capacity), jnp.float32),
        ],
        axis=1,
    )[:, None, :]
    packed = jnp.concatenate([send_values.reshape(blocks, capacity, channels), side], axis=1)
    got = lax.all_to_all(packed, "col", split_axis=0, concat_axis=0, tiled=True)
    got_values = got[:, :capacity, :].reshape(total_slots, channels)
    got_cells = got[:, capacity, :capacity].reshape(total_slots).astype(jnp.int32)
    got_marks = got[:, capacity, capacity : 2 * capacity].reshape(total_slots)
    obs_index = got_cells
    obs_gain = got_marks[:, None] * obs_weights[None, :]

    placement = (
        obs_index[None, :] == jnp.arange(rows_here * columns, dtype=jnp.int32)[:, None]
    ).astype(jnp.float32)

    def spread_back(weighted):
        back = jnp.dot(weighted, obs_jacobian.T, precision=lax.Precision.HIGHEST)
        grid = jnp.dot(placement, back, precision=lax.Precision.HIGHEST)
        return grid.reshape(rows_here, columns, features)

    def adjoint_parts(gradient):
        own_gradient = lax.dynamic_slice_in_dim(gradient, offset, quarter, 1)
        rounded = gradient.astype(jnp.bfloat16)
        static = jnp.dot(
            own_gradient.reshape(rows_here * quarter, features),
            static_root.T,
            precision=lax.Precision.HIGHEST,
        ).reshape(rows_here, quarter, features)
        projected = jnp.einsum(
            "kyxf,yxf->kyx", perturbations, rounded, preferred_element_type=jnp.float32
        )
        return static, projected

    def forward_partial(static_part, smoothed_field):
        smoothed = smoothed_field.astype(jnp.bfloat16)
        partial_sum = jnp.einsum(
            "kyxf,kyx->yxf", perturbations, smoothed, preferred_element_type=jnp.float32
        )
        forward_static = jnp.dot(
            static_part.reshape(rows_here * quarter, features),
            static_root,
            precision=lax.Precision.HIGHEST,
        ).reshape(rows_here, quarter, features)
        own_slice = lax.dynamic_slice_in_dim(partial_sum, offset, quarter, 1) + forward_static
        return lax.dynamic_update_slice_in_dim(partial_sum, own_slice, offset, 1)

    cell_x = obs_index % columns
    in_quarter = (cell_x >= offset) & (cell_x < offset + quarter)
    quarter_index = jnp.where(in_quarter, (obs_index // columns) * quarter + cell_x - offset, 0)
    quarter_gain = jnp.where(in_quarter[:, None], obs_gain, 0.0)
    quarter_placement = (
        (quarter_index[None, :] == jnp.arange(rows_here * quarter, dtype=jnp.int32)[:, None])
        & in_quarter[None, :]
    ).astype(jnp.float32)

    def observed(partial_sum):
        pieces = jnp.moveaxis(partial_sum.reshape(rows_here, parts, quarter, features), 1, 0)
        own_image = jnp.sum(lax.all_to_all(pieces, "mem", 0, 0, tiled=True), axis=0)
        gathered = own_image.reshape(rows_here * quarter, features)[quarter_index]
        model_obs = jnp.dot(gathered, obs_jacobian, precision=lax.Precision.HIGHEST)
        return own_image, model_obs

    def observed_adjoint(model_obs):
        back = jnp.dot(quarter_gain * model_obs, obs_jacobian.T, precision=lax.Precision.HIGHEST)
        own_gradient = jnp.dot(quarter_placement, back, precision=lax.Precision.HIGHEST)
        static = jnp.dot(own_gradient, static_root.T, precision=lax.Precision.HIGHEST).reshape(
            rows_here, quarter, features
        )
        rounded = own_gradient.reshape(rows_here, quarter, features).astype(jnp.bfloat16)
        spread = jnp.broadcast_to(rounded[None], (parts,) + rounded.shape)
        quarters = lax.all_to_all(spread, "mem", 0, 0, tiled=True)
        rounded = jnp.moveaxis(quarters, 0, 1).reshape(rows_here, columns, features)
        projected = jnp.einsum(
            "kyxf,yxf->kyx", perturbations, rounded, preferred_element_type=jnp.float32
        )
        return static, projected

    right_static, right_projected = adjoint_parts(spread_back(obs_gain * got_values))
    wide = sweep_steps(neighbours(right_projected, "col", 1, 2), coeffs_wide, NSWEEP)
    right_ensemble = wide[:, 2 * rows_here : 3 * rows_here]
    wide = sweep_steps(wide, coeffs_wide, NSWEEP)
    smoothed_right = wide[:, 2 * rows_here : 3 * rows_here]
    direction = (right_static, right_ensemble)

    partial0 = forward_partial(right_static, smoothed_right)
    own_image0, model_obs = observed(partial0)
    adj_static, adj_projected = observed_adjoint(model_obs)
    image = (right_static + adj_static, right_ensemble + sweeps(adj_projected, coeffs))
    sums = global_sum(
        jnp.stack(
            [
                local_inner(direction, direction),
                local_inner(direction, image),
                local_inner(image, image),
            ]
        )
    )
    smoothed_image = sweeps(image[1], coeffs)
    norm_now, curve, image_norm = sums[0], sums[1], sums[2]
    step0 = norm_now / curve
    state = (step0 * direction[0], step0 * direction[1])
    residual = (direction[0] - step0 * image[0], direction[1] - step0 * image[1])
    norm_next = norm_now - 2.0 * step0 * curve + step0 * step0 * image_norm
    ratio = norm_next / norm_now
    direction = (residual[0] + ratio * direction[0], residual[1] + ratio * direction[1])
    smoothed_direction = (smoothed_right - step0 * smoothed_image) + ratio * smoothed_right
    norm_now = norm_next

    partial1 = forward_partial(direction[0], smoothed_direction)
    own_image1, model_obs = observed(partial1)
    curve = (
        jnp.sum(direction[0] * direction[0])
        + jnp.sum(direction[1] * direction[1])
        + jnp.sum(quarter_gain * model_obs * model_obs)
    )
    step1 = norm_now / global_sum(curve)
    state = (state[0] + step1 * direction[0], state[1] + step1 * direction[1])

    increment = step0 * own_image0 + step1 * own_image1
    return (increment, state[0], state[1])


def solution(mesh):
    placed = (
        P("mem", "col", None, None),
        P(),
        P(),
        P("col", None),
        P(),
        P("col", None),
        P("col", None),
        P("col"),
        P("col"),
    )
    return jax.shard_map(
        shards,
        mesh=mesh,
        in_specs=placed,
        out_specs=(P("col", "mem", None), P("col", "mem", None), P("mem", "col", None)),
        check_vma=False,
    )
```

```python
import jax
import jax.numpy as jnp
from jax import lax
from jax.sharding import PartitionSpec as P

NSWEEP = 4
ITERS = 2


def neighbours(block, axis, dim, reach):
    count = lax.axis_size(axis)
    below, above = [], []
    for shift in range(1, reach + 1):
        forward = [(i, i + shift) for i in range(count - shift)]
        backward = [(target, source) for source, target in forward]
        below.insert(0, lax.ppermute(block, axis, forward))
        above.append(lax.ppermute(block, axis, backward))
    return jnp.concatenate(below + [block] + above, axis=dim)


def face_coefficients(length_scale, reach):
    rimmed = neighbours(length_scale, "col", 0, reach)
    padded = jnp.pad(rimmed, ((1, 1), (1, 1)))
    centre = padded[1:-1, 1:-1]
    return (
        jnp.sqrt(centre * padded[:-2, 1:-1]),
        jnp.sqrt(centre * padded[2:, 1:-1]),
        jnp.sqrt(centre * padded[1:-1, :-2]),
        jnp.sqrt(centre * padded[1:-1, 2:]),
    )


def sweep_steps(values, coeffs, count):
    face_up, face_down, face_left, face_right = coeffs
    for sweep_step in range(count):
        padded = jnp.pad(values, ((0, 0), (1, 1), (1, 1)))
        centre = values
        values = (
            centre
            + face_up * (padded[:, :-2, 1:-1] - centre)
            + face_down * (padded[:, 2:, 1:-1] - centre)
            + face_left * (padded[:, 1:-1, :-2] - centre)
            + face_right * (padded[:, 1:-1, 2:] - centre)
        )
    return values


def global_sum(values):
    axes = ("mem", "col")
    count = lax.axis_size(axes)
    spread = jnp.broadcast_to(values[None], (count,) + values.shape)
    return jnp.sum(lax.all_to_all(spread, axes, 0, 0, tiled=True), axis=0)


def local_inner(first, second):
    return jnp.sum(first[0] * second[0]) + jnp.sum(first[1] * second[1])


def shards(
    perturbations,
    static_root,
    obs_jacobian,
    innovations,
    obs_weights,
    length_scale,
    obs_owner,
    obs_cell,
    obs_count,
):
    members, rows_here, columns, features = perturbations.shape
    parts = lax.axis_size("mem")
    quarter = columns // parts
    offset = lax.axis_index("mem") * quarter
    blocks = lax.axis_size("col")
    obs_dev, channels = innovations.shape
    capacity = max(2, 2 * obs_dev // blocks)
    total_slots = blocks * capacity
    coeffs_wide = face_coefficients(length_scale, 2)
    is_live = jnp.arange(obs_dev, dtype=jnp.int32) < obs_count[0]
    owner_ids = obs_owner[:, 0]
    onehot = (
        (owner_ids[:, None] == jnp.arange(blocks, dtype=jnp.int32)[None, :]) & is_live[:, None]
    ).astype(jnp.int32)
    slot_rank = jnp.sum((jnp.cumsum(onehot, axis=0) - onehot) * onehot, axis=1)
    slot_ids = jnp.where(is_live, owner_ids * capacity + slot_rank, total_slots)
    send_values = (
        jnp.zeros((total_slots, channels), jnp.float32).at[slot_ids].set(innovations, mode="drop")
    )
    tags = jnp.stack([obs_cell.astype(jnp.float32), jnp.ones((obs_dev,), jnp.float32)], axis=1)
    tags = jnp.zeros((total_slots, 2), jnp.float32).at[slot_ids].set(tags, mode="drop")
    side = jnp.concatenate(
        [
            jnp.swapaxes(tags.reshape(blocks, capacity, 2), 1, 2).reshape(blocks, 2 * capacity),
            jnp.zeros((blocks, channels - 2 * capacity), jnp.float32),
        ],
        axis=1,
    )[:, None, :]
    packed = jnp.concatenate([send_values.reshape(blocks, capacity, channels), side], axis=1)
    got = lax.all_to_all(packed, "col", split_axis=0, concat_axis=0, tiled=True)
    got_values = got[:, :capacity, :].reshape(total_slots, channels)
    got_cells = got[:, capacity, :capacity].reshape(total_slots).astype(jnp.int32)
    got_marks = got[:, capacity, capacity : 2 * capacity].reshape(total_slots)
    obs_index = got_cells
    obs_gain = got_marks[:, None] * obs_weights[None, :]

    placement = (
        obs_index[None, :] == jnp.arange(rows_here * columns, dtype=jnp.int32)[:, None]
    ).astype(jnp.float32)

    def spread_back(weighted):
        back = jnp.dot(weighted, obs_jacobian.T, precision=lax.Precision.HIGHEST)
        grid = jnp.dot(placement, back, precision=lax.Precision.HIGHEST)
        return grid.reshape(rows_here, columns, features)

    def adjoint_parts(gradient):
        own_gradient = lax.dynamic_slice_in_dim(gradient, offset, quarter, 1)
        rounded = gradient.astype(jnp.bfloat16)
        static = jnp.dot(
            own_gradient.reshape(rows_here * quarter, features),
            static_root.T,
            precision=lax.Precision.HIGHEST,
        ).reshape(rows_here, quarter, features)
        projected = jnp.einsum(
            "kyxf,yxf->kyx", perturbations, rounded, preferred_element_type=jnp.float32
        )
        return static, projected

    def forward_partial(static_part, smoothed_field):
        smoothed = smoothed_field.astype(jnp.bfloat16)
        partial_sum = jnp.einsum(
            "kyxf,kyx->yxf", perturbations, smoothed, preferred_element_type=jnp.float32
        )
        forward_static = jnp.dot(
            static_part.reshape(rows_here * quarter, features),
            static_root,
            precision=lax.Precision.HIGHEST,
        ).reshape(rows_here, quarter, features)
        own_slice = lax.dynamic_slice_in_dim(partial_sum, offset, quarter, 1) + forward_static
        return lax.dynamic_update_slice_in_dim(partial_sum, own_slice, offset, 1)

    cell_x = obs_index % columns
    in_quarter = (cell_x >= offset) & (cell_x < offset + quarter)
    quarter_index = jnp.where(in_quarter, (obs_index // columns) * quarter + cell_x - offset, 0)
    quarter_gain = jnp.where(in_quarter[:, None], obs_gain, 0.0)
    quarter_placement = (
        (quarter_index[None, :] == jnp.arange(rows_here * quarter, dtype=jnp.int32)[:, None])
        & in_quarter[None, :]
    ).astype(jnp.float32)

    def observed(partial_sum):
        pieces = jnp.moveaxis(partial_sum.reshape(rows_here, parts, quarter, features), 1, 0)
        own_image = jnp.sum(lax.all_to_all(pieces, "mem", 0, 0, tiled=True), axis=0)
        gathered = own_image.reshape(rows_here * quarter, features)[quarter_index]
        model_obs = jnp.dot(gathered, obs_jacobian, precision=lax.Precision.HIGHEST)
        return own_image, model_obs

    def observed_adjoint(model_obs):
        back = jnp.dot(quarter_gain * model_obs, obs_jacobian.T, precision=lax.Precision.HIGHEST)
        own_gradient = jnp.dot(quarter_placement, back, precision=lax.Precision.HIGHEST)
        static = jnp.dot(own_gradient, static_root.T, precision=lax.Precision.HIGHEST).reshape(
            rows_here, quarter, features
        )
        rounded = own_gradient.reshape(rows_here, quarter, features).astype(jnp.bfloat16)
        spread = jnp.broadcast_to(rounded[None], (parts,) + rounded.shape)
        quarters = lax.all_to_all(spread, "mem", 0, 0, tiled=True)
        rounded = jnp.moveaxis(quarters, 0, 1).reshape(rows_here, columns, features)
        projected = jnp.einsum(
            "kyxf,yxf->kyx", perturbations, rounded, preferred_element_type=jnp.float32
        )
        return static, projected

    right_static, right_projected = adjoint_parts(spread_back(obs_gain * got_values))
    wide = sweep_steps(neighbours(right_projected, "col", 1, 2), coeffs_wide, NSWEEP)
    right_ensemble = wide[:, 2 * rows_here : 3 * rows_here]
    wide = sweep_steps(wide, coeffs_wide, NSWEEP)
    smoothed_right = wide[:, 2 * rows_here : 3 * rows_here]
    direction = (right_static, right_ensemble)

    partial0 = forward_partial(right_static, smoothed_right)
    own_image0, model_obs = observed(partial0)
    adj_static, adj_projected = observed_adjoint(model_obs)
    wide = sweep_steps(neighbours(adj_projected, "col", 1, 2), coeffs_wide, NSWEEP)
    smoothed_adjoint = wide[:, 2 * rows_here : 3 * rows_here]
    wide = sweep_steps(wide, coeffs_wide, NSWEEP)
    smoothed_image = smoothed_right + wide[:, 2 * rows_here : 3 * rows_here]
    image = (right_static + adj_static, right_ensemble + smoothed_adjoint)
    sums = global_sum(
        jnp.stack(
            [
                local_inner(direction, direction),
                local_inner(direction, image),
                local_inner(image, image),
            ]
        )
    )
    norm_now, curve, image_norm = sums[0], sums[1], sums[2]
    step0 = norm_now / curve
    state = (step0 * direction[0], step0 * direction[1])
    residual = (direction[0] - step0 * image[0], direction[1] - step0 * image[1])
    norm_next = norm_now - 2.0 * step0 * curve + step0 * step0 * image_norm
    ratio = norm_next / norm_now
    direction = (residual[0] + ratio * direction[0], residual[1] + ratio * direction[1])
    smoothed_direction = (smoothed_right - step0 * smoothed_image) + ratio * smoothed_right
    norm_now = norm_next

    partial1 = forward_partial(direction[0], smoothed_direction)
    own_image1, model_obs = observed(partial1)
    curve = (
        jnp.sum(direction[0] * direction[0])
        + jnp.sum(direction[1] * direction[1])
        + jnp.sum(quarter_gain * model_obs * model_obs)
    )
    step1 = norm_now / global_sum(curve)
    state = (state[0] + step1 * direction[0], state[1] + step1 * direction[1])

    increment = step0 * own_image0 + step1 * own_image1
    return (increment, state[0], state[1])


def solution(mesh):
    placed = (
        P("mem", "col", None, None),
        P(),
        P(),
        P("col", None),
        P(),
        P("col", None),
        P("col", None),
        P("col"),
        P("col"),
    )
    return jax.shard_map(
        shards,
        mesh=mesh,
        in_specs=placed,
        out_specs=(P("col", "mem", None), P("col", "mem", None), P("mem", "col", None)),
        check_vma=False,
    )
```

```python
import jax
import jax.numpy as jnp
from jax import lax
from jax.sharding import PartitionSpec as P

NSWEEP = 4
ITERS = 2


def neighbours(block, axis, dim, reach):
    count = lax.axis_size(axis)
    below, above = [], []
    for shift in range(1, reach + 1):
        forward = [(i, i + shift) for i in range(count - shift)]
        backward = [(target, source) for source, target in forward]
        below.insert(0, lax.ppermute(block, axis, forward))
        above.append(lax.ppermute(block, axis, backward))
    return jnp.concatenate(below + [block] + above, axis=dim)


def face_coefficients(length_scale, reach):
    rimmed = neighbours(length_scale, "col", 0, reach)
    padded = jnp.pad(rimmed, ((1, 1), (1, 1)))
    centre = padded[1:-1, 1:-1]
    return (
        jnp.sqrt(centre * padded[:-2, 1:-1]),
        jnp.sqrt(centre * padded[2:, 1:-1]),
        jnp.sqrt(centre * padded[1:-1, :-2]),
        jnp.sqrt(centre * padded[1:-1, 2:]),
    )


def sweep_steps(values, coeffs, count):
    face_up, face_down, face_left, face_right = coeffs
    for sweep_step in range(count):
        padded = jnp.pad(values, ((0, 0), (1, 1), (1, 1)))
        centre = values
        values = (
            centre
            + face_up * (padded[:, :-2, 1:-1] - centre)
            + face_down * (padded[:, 2:, 1:-1] - centre)
            + face_left * (padded[:, 1:-1, :-2] - centre)
            + face_right * (padded[:, 1:-1, 2:] - centre)
        )
    return values


def sweeps(values, coeffs):
    rows = values.shape[1]
    done = sweep_steps(neighbours(values, "col", 1, 1), coeffs, NSWEEP)
    return done[:, rows : 2 * rows]


def global_sum(values):
    axes = ("mem", "col")
    count = lax.axis_size(axes)
    spread = jnp.broadcast_to(values[None], (count,) + values.shape)
    return jnp.sum(lax.all_to_all(spread, axes, 0, 0, tiled=True), axis=0)


def local_inner(first, second):
    return jnp.sum(first[0] * second[0]) + jnp.sum(first[1] * second[1])


def shards(
    perturbations,
    static_root,
    obs_jacobian,
    innovations,
    obs_weights,
    length_scale,
    obs_owner,
    obs_cell,
    obs_count,
):
    members, rows_here, columns, features = perturbations.shape
    parts = lax.axis_size("mem")
    quarter = columns // parts
    offset = lax.axis_index("mem") * quarter
    blocks = lax.axis_size("col")
    obs_dev, channels = innovations.shape
    capacity = max(2, 2 * obs_dev // blocks)
    total_slots = blocks * capacity
    coeffs_wide = face_coefficients(length_scale, 2)
    coeffs = tuple(face[rows_here : 4 * rows_here] for face in coeffs_wide)
    is_live = jnp.arange(obs_dev, dtype=jnp.int32) < obs_count[0]
    owner_ids = obs_owner[:, 0]
    onehot = (
        (owner_ids[:, None] == jnp.arange(blocks, dtype=jnp.int32)[None, :]) & is_live[:, None]
    ).astype(jnp.int32)
    slot_rank = jnp.sum((jnp.cumsum(onehot, axis=0) - onehot) * onehot, axis=1)
    slot_ids = jnp.where(is_live, owner_ids * capacity + slot_rank, total_slots)
    send_values = (
        jnp.zeros((total_slots, channels), jnp.float32).at[slot_ids].set(innovations, mode="drop")
    )
    tags = jnp.stack([obs_cell.astype(jnp.float32), jnp.ones((obs_dev,), jnp.float32)], axis=1)
    tags = jnp.zeros((total_slots, 2), jnp.float32).at[slot_ids].set(tags, mode="drop")
    side = jnp.concatenate(
        [
            jnp.swapaxes(tags.reshape(blocks, capacity, 2), 1, 2).reshape(blocks, 2 * capacity),
            jnp.zeros((blocks, channels - 2 * capacity), jnp.float32),
        ],
        axis=1,
    )[:, None, :]
    packed = jnp.concatenate([send_values.reshape(blocks, capacity, channels), side], axis=1)
    got = lax.all_to_all(packed, "col", split_axis=0, concat_axis=0, tiled=True)
    got_values = got[:, :capacity, :].reshape(total_slots, channels)
    got_cells = got[:, capacity, :capacity].reshape(total_slots).astype(jnp.int32)
    got_marks = got[:, capacity, capacity : 2 * capacity].reshape(total_slots)
    obs_index = got_cells
    obs_gain = got_marks[:, None] * obs_weights[None, :]

    placement = (
        obs_index[None, :] == jnp.arange(rows_here * columns, dtype=jnp.int32)[:, None]
    ).astype(jnp.float32)

    def spread_back(weighted):
        back = jnp.dot(weighted, obs_jacobian.T, precision=lax.Precision.HIGHEST)
        grid = jnp.dot(placement, back, precision=lax.Precision.HIGHEST)
        return grid.reshape(rows_here, columns, features)

    def adjoint_parts(gradient):
        own_gradient = lax.dynamic_slice_in_dim(gradient, offset, quarter, 1)
        rounded = gradient.astype(jnp.bfloat16)
        static = jnp.dot(
            own_gradient.reshape(rows_here * quarter, features),
            static_root.T,
            precision=lax.Precision.HIGHEST,
        ).reshape(rows_here, quarter, features)
        projected = jnp.einsum(
            "kyxf,yxf->kyx", perturbations, rounded, preferred_element_type=jnp.float32
        )
        return static, projected

    def forward_partial(static_part, smoothed_field):
        smoothed = smoothed_field.astype(jnp.bfloat16)
        partial_sum = jnp.einsum(
            "kyxf,kyx->yxf", perturbations, smoothed, preferred_element_type=jnp.float32
        )
        forward_static = jnp.dot(
            static_part.reshape(rows_here * quarter, features),
            static_root,
            precision=lax.Precision.HIGHEST,
        ).reshape(rows_here, quarter, features)
        own_slice = lax.dynamic_slice_in_dim(partial_sum, offset, quarter, 1) + forward_static
        return lax.dynamic_update_slice_in_dim(partial_sum, own_slice, offset, 1)

    cell_x = obs_index % columns
    in_quarter = (cell_x >= offset) & (cell_x < offset + quarter)
    quarter_index = jnp.where(in_quarter, (obs_index // columns) * quarter + cell_x - offset, 0)
    quarter_gain = jnp.where(in_quarter[:, None], obs_gain, 0.0)
    quarter_placement = (
        (quarter_index[None, :] == jnp.arange(rows_here * quarter, dtype=jnp.int32)[:, None])
        & in_quarter[None, :]
    ).astype(jnp.float32)

    def observed(partial_sum):
        pieces = jnp.moveaxis(partial_sum.reshape(rows_here, parts, quarter, features), 1, 0)
        own_image = jnp.sum(lax.all_to_all(pieces, "mem", 0, 0, tiled=True), axis=0)
        gathered = own_image.reshape(rows_here * quarter, features)[quarter_index]
        model_obs = jnp.dot(gathered, obs_jacobian, precision=lax.Precision.HIGHEST)
        return own_image, model_obs

    def observed_adjoint(model_obs):
        back = jnp.dot(quarter_gain * model_obs, obs_jacobian.T, precision=lax.Precision.HIGHEST)
        own_gradient = jnp.dot(quarter_placement, back, precision=lax.Precision.HIGHEST)
        static = jnp.dot(own_gradient, static_root.T, precision=lax.Precision.HIGHEST).reshape(
            rows_here, quarter, features
        )
        rounded = own_gradient.reshape(rows_here, quarter, features).astype(jnp.bfloat16)
        spread = jnp.broadcast_to(rounded[None], (parts,) + rounded.shape)
        quarters = lax.all_to_all(spread, "mem", 0, 0, tiled=True)
        rounded = jnp.moveaxis(quarters, 0, 1).reshape(rows_here, columns, features)
        projected = jnp.einsum(
            "kyxf,yxf->kyx", perturbations, rounded, preferred_element_type=jnp.float32
        )
        return static, projected

    right_static, right_projected = adjoint_parts(spread_back(obs_gain * got_values))
    wide = sweep_steps(neighbours(right_projected, "col", 1, 2), coeffs_wide, NSWEEP)
    right_ensemble = wide[:, 2 * rows_here : 3 * rows_here]
    wide = sweep_steps(wide, coeffs_wide, NSWEEP)
    smoothed_right = wide[:, 2 * rows_here : 3 * rows_here]
    direction = (right_static, right_ensemble)

    partial0 = forward_partial(right_static, smoothed_right)
    own_image0, model_obs = observed(partial0)
    adj_static, adj_projected = observed_adjoint(model_obs)
    image = (right_static + adj_static, right_ensemble + sweeps(adj_projected, coeffs))
    local_sums = jnp.stack(
        [
            local_inner(direction, direction),
            local_inner(direction, image),
            local_inner(image, image),
        ]
    )
    rimmed, local_sums = lax.optimization_barrier((neighbours(image[1], "col", 1, 1), local_sums))
    sums = global_sum(local_sums)
    smoothed_image = sweep_steps(rimmed, coeffs, NSWEEP)[:, rows_here : 2 * rows_here]
    norm_now, curve, image_norm = sums[0], sums[1], sums[2]
    step0 = norm_now / curve
    state = (step0 * direction[0], step0 * direction[1])
    residual = (direction[0] - step0 * image[0], direction[1] - step0 * image[1])
    norm_next = norm_now - 2.0 * step0 * curve + step0 * step0 * image_norm
    ratio = norm_next / norm_now
    direction = (residual[0] + ratio * direction[0], residual[1] + ratio * direction[1])
    smoothed_direction = (smoothed_right - step0 * smoothed_image) + ratio * smoothed_right
    norm_now = norm_next

    partial1 = forward_partial(direction[0], smoothed_direction)
    own_image1, model_obs = observed(partial1)
    curve = (
        jnp.sum(direction[0] * direction[0])
        + jnp.sum(direction[1] * direction[1])
        + jnp.sum(quarter_gain * model_obs * model_obs)
    )
    step1 = norm_now / global_sum(curve)
    state = (state[0] + step1 * direction[0], state[1] + step1 * direction[1])

    increment = step0 * own_image0 + step1 * own_image1
    return (increment, state[0], state[1])


def solution(mesh):
    placed = (
        P("mem", "col", None, None),
        P(),
        P(),
        P("col", None),
        P(),
        P("col", None),
        P("col", None),
        P("col"),
        P("col"),
    )
    return jax.shard_map(
        shards,
        mesh=mesh,
        in_specs=placed,
        out_specs=(P("col", "mem", None), P("col", "mem", None), P("mem", "col", None)),
        check_vma=False,
    )
```

```python
import jax
import jax.numpy as jnp
from jax import lax
from jax.sharding import PartitionSpec as P

NSWEEP = 4
ITERS = 2


def neighbours(block, axis, dim, reach):
    count = lax.axis_size(axis)
    below, above = [], []
    for shift in range(1, reach + 1):
        forward = [(i, i + shift) for i in range(count - shift)]
        backward = [(target, source) for source, target in forward]
        below.insert(0, lax.ppermute(block, axis, forward))
        above.append(lax.ppermute(block, axis, backward))
    return jnp.concatenate(below + [block] + above, axis=dim)


def face_coefficients(length_scale, reach):
    rimmed = neighbours(length_scale, "col", 0, reach)
    padded = jnp.pad(rimmed, ((1, 1), (1, 1)))
    centre = padded[1:-1, 1:-1]
    return (
        jnp.sqrt(centre * padded[:-2, 1:-1]),
        jnp.sqrt(centre * padded[2:, 1:-1]),
        jnp.sqrt(centre * padded[1:-1, :-2]),
        jnp.sqrt(centre * padded[1:-1, 2:]),
    )


def sweep_steps(values, coeffs, count):
    face_up, face_down, face_left, face_right = coeffs
    for sweep_step in range(count):
        padded = jnp.pad(values, ((0, 0), (1, 1), (1, 1)))
        centre = values
        values = (
            centre
            + face_up * (padded[:, :-2, 1:-1] - centre)
            + face_down * (padded[:, 2:, 1:-1] - centre)
            + face_left * (padded[:, 1:-1, :-2] - centre)
            + face_right * (padded[:, 1:-1, 2:] - centre)
        )
    return values


def sweeps(values, coeffs):
    rows = values.shape[1]
    done = sweep_steps(neighbours(values, "col", 1, 1), coeffs, NSWEEP)
    return done[:, rows : 2 * rows]


def global_sum(values):
    axes = ("mem", "col")
    count = lax.axis_size(axes)
    spread = jnp.broadcast_to(values[None], (count,) + values.shape)
    return jnp.sum(lax.all_to_all(spread, axes, 0, 0, tiled=True), axis=0)


def local_inner(first, second):
    return jnp.sum(first[0] * second[0]) + jnp.sum(first[1] * second[1])


def shards(
    perturbations,
    static_root,
    obs_jacobian,
    innovations,
    obs_weights,
    length_scale,
    obs_owner,
    obs_cell,
    obs_count,
):
    members, rows_here, columns, features = perturbations.shape
    parts = lax.axis_size("mem")
    quarter = columns // parts
    offset = lax.axis_index("mem") * quarter
    blocks = lax.axis_size("col")
    obs_dev, channels = innovations.shape
    capacity = max(2, 2 * obs_dev // blocks)
    total_slots = blocks * capacity
    coeffs_wide = face_coefficients(length_scale, 2)
    coeffs = tuple(face[rows_here : 4 * rows_here] for face in coeffs_wide)
    is_live = jnp.arange(obs_dev, dtype=jnp.int32) < obs_count[0]
    owner_ids = obs_owner[:, 0]
    onehot = (
        (owner_ids[:, None] == jnp.arange(blocks, dtype=jnp.int32)[None, :]) & is_live[:, None]
    ).astype(jnp.int32)
    slot_rank = jnp.sum((jnp.cumsum(onehot, axis=0) - onehot) * onehot, axis=1)
    slot_ids = jnp.where(is_live, owner_ids * capacity + slot_rank, total_slots)
    send_values = (
        jnp.zeros((total_slots, channels), jnp.float32).at[slot_ids].set(innovations, mode="drop")
    )
    tags = jnp.stack([obs_cell.astype(jnp.float32), jnp.ones((obs_dev,), jnp.float32)], axis=1)
    tags = jnp.zeros((total_slots, 2), jnp.float32).at[slot_ids].set(tags, mode="drop")
    side = jnp.concatenate(
        [
            jnp.swapaxes(tags.reshape(blocks, capacity, 2), 1, 2).reshape(blocks, 2 * capacity),
            jnp.zeros((blocks, channels - 2 * capacity), jnp.float32),
        ],
        axis=1,
    )[:, None, :]
    packed = jnp.concatenate([send_values.reshape(blocks, capacity, channels), side], axis=1)
    got = lax.all_to_all(packed, "col", split_axis=0, concat_axis=0, tiled=True)
    got_values = got[:, :capacity, :].reshape(total_slots, channels)
    got_cells = got[:, capacity, :capacity].reshape(total_slots).astype(jnp.int32)
    got_marks = got[:, capacity, capacity : 2 * capacity].reshape(total_slots)
    obs_index = got_cells
    obs_gain = got_marks[:, None] * obs_weights[None, :]

    placement = (
        obs_index[None, :] == jnp.arange(rows_here * columns, dtype=jnp.int32)[:, None]
    ).astype(jnp.float32)

    def spread_back(weighted):
        back = jnp.dot(weighted, obs_jacobian.T, precision=lax.Precision.HIGHEST)
        grid = jnp.dot(placement, back, precision=lax.Precision.HIGHEST)
        return grid.reshape(rows_here, columns, features)

    def adjoint_parts(gradient):
        own_gradient = lax.dynamic_slice_in_dim(gradient, offset, quarter, 1)
        rounded = gradient.astype(jnp.bfloat16)
        static = jnp.dot(
            own_gradient.reshape(rows_here * quarter, features),
            static_root.T,
            precision=lax.Precision.HIGHEST,
        ).reshape(rows_here, quarter, features)
        projected = jnp.einsum(
            "kyxf,yxf->kyx", perturbations, rounded, preferred_element_type=jnp.float32
        )
        return static, projected

    split_perturbations = perturbations.reshape(members, rows_here, parts, quarter, features)
    mem_index = lax.axis_index("mem")

    def forward_partial(static_part, smoothed_field):
        smoothed = smoothed_field.astype(jnp.bfloat16).reshape(members, rows_here, parts, quarter)
        partial_sum = jnp.einsum(
            "kyqxf,kyqx->qyxf", split_perturbations, smoothed, preferred_element_type=jnp.float32
        )
        forward_static = jnp.dot(
            static_part.reshape(rows_here * quarter, features),
            static_root,
            precision=lax.Precision.HIGHEST,
        ).reshape(rows_here, quarter, features)
        own_slice = lax.dynamic_index_in_dim(partial_sum, mem_index, 0, keepdims=False) + forward_static
        return lax.dynamic_update_index_in_dim(partial_sum, own_slice, mem_index, 0)

    cell_x = obs_index % columns
    in_quarter = (cell_x >= offset) & (cell_x < offset + quarter)
    quarter_index = jnp.where(in_quarter, (obs_index // columns) * quarter + cell_x - offset, 0)
    quarter_gain = jnp.where(in_quarter[:, None], obs_gain, 0.0)
    quarter_placement = (
        (quarter_index[None, :] == jnp.arange(rows_here * quarter, dtype=jnp.int32)[:, None])
        & in_quarter[None, :]
    ).astype(jnp.float32)

    def observed(partial_sum):
        own_image = jnp.sum(lax.all_to_all(partial_sum, "mem", 0, 0, tiled=True), axis=0)
        gathered = own_image.reshape(rows_here * quarter, features)[quarter_index]
        model_obs = jnp.dot(gathered, obs_jacobian, precision=lax.Precision.HIGHEST)
        return own_image, model_obs

    def observed_adjoint(model_obs):
        back = jnp.dot(quarter_gain * model_obs, obs_jacobian.T, precision=lax.Precision.HIGHEST)
        own_gradient = jnp.dot(quarter_placement, back, precision=lax.Precision.HIGHEST)
        static = jnp.dot(own_gradient, static_root.T, precision=lax.Precision.HIGHEST).reshape(
            rows_here, quarter, features
        )
        rounded = own_gradient.reshape(rows_here, quarter, features).astype(jnp.bfloat16)
        spread = jnp.broadcast_to(rounded[None], (parts,) + rounded.shape)
        quarters = lax.all_to_all(spread, "mem", 0, 0, tiled=True)
        projected = jnp.einsum(
            "kyqxf,qyxf->kyqx", split_perturbations, quarters, preferred_element_type=jnp.float32
        ).reshape(members, rows_here, columns)
        return static, projected

    right_static, right_projected = adjoint_parts(spread_back(obs_gain * got_values))
    wide = sweep_steps(neighbours(right_projected, "col", 1, 2), coeffs_wide, NSWEEP)
    right_ensemble = wide[:, 2 * rows_here : 3 * rows_here]
    wide = sweep_steps(wide, coeffs_wide, NSWEEP)
    smoothed_right = wide[:, 2 * rows_here : 3 * rows_here]
    direction = (right_static, right_ensemble)

    partial0 = forward_partial(right_static, smoothed_right)
    own_image0, model_obs = observed(partial0)
    adj_static, adj_projected = observed_adjoint(model_obs)
    image = (right_static + adj_static, right_ensemble + sweeps(adj_projected, coeffs))
    sums = global_sum(
        jnp.stack(
            [
                local_inner(direction, direction),
                local_inner(direction, image),
                local_inner(image, image),
            ]
        )
    )
    smoothed_image = sweeps(image[1], coeffs)
    norm_now, curve, image_norm = sums[0], sums[1], sums[2]
    step0 = norm_now / curve
    state = (step0 * direction[0], step0 * direction[1])
    residual = (direction[0] - step0 * image[0], direction[1] - step0 * image[1])
    norm_next = norm_now - 2.0 * step0 * curve + step0 * step0 * image_norm
    ratio = norm_next / norm_now
    direction = (residual[0] + ratio * direction[0], residual[1] + ratio * direction[1])
    smoothed_direction = (smoothed_right - step0 * smoothed_image) + ratio * smoothed_right
    norm_now = norm_next

    partial1 = forward_partial(direction[0], smoothed_direction)
    own_image1, model_obs = observed(partial1)
    curve = (
        jnp.sum(direction[0] * direction[0])
        + jnp.sum(direction[1] * direction[1])
        + jnp.sum(quarter_gain * model_obs * model_obs)
    )
    step1 = norm_now / global_sum(curve)
    state = (state[0] + step1 * direction[0], state[1] + step1 * direction[1])

    increment = step0 * own_image0 + step1 * own_image1
    return (increment, state[0], state[1])


def solution(mesh):
    placed = (
        P("mem", "col", None, None),
        P(),
        P(),
        P("col", None),
        P(),
        P("col", None),
        P("col", None),
        P("col"),
        P("col"),
    )
    return jax.shard_map(
        shards,
        mesh=mesh,
        in_specs=placed,
        out_specs=(P("col", "mem", None), P("col", "mem", None), P("mem", "col", None)),
        check_vma=False,
    )
```

```python
import jax
import jax.numpy as jnp
from jax import lax
from jax.sharding import PartitionSpec as P

NSWEEP = 4
ITERS = 2


def neighbours(block, axis, dim, reach):
    count = lax.axis_size(axis)
    below, above = [], []
    for shift in range(1, reach + 1):
        forward = [(i, i + shift) for i in range(count - shift)]
        backward = [(target, source) for source, target in forward]
        below.insert(0, lax.ppermute(block, axis, forward))
        above.append(lax.ppermute(block, axis, backward))
    return jnp.concatenate(below + [block] + above, axis=dim)


def face_coefficients(length_scale, reach):
    rimmed = neighbours(length_scale, "col", 0, reach)
    padded = jnp.pad(rimmed, ((1, 1), (1, 1)))
    centre = padded[1:-1, 1:-1]
    return (
        jnp.sqrt(centre * padded[:-2, 1:-1]),
        jnp.sqrt(centre * padded[2:, 1:-1]),
        jnp.sqrt(centre * padded[1:-1, :-2]),
        jnp.sqrt(centre * padded[1:-1, 2:]),
    )


def sweep_steps(values, coeffs, count):
    face_up, face_down, face_left, face_right = coeffs
    for sweep_step in range(count):
        padded = jnp.pad(values, ((0, 0), (1, 1), (1, 1)))
        centre = values
        values = (
            centre
            + face_up * (padded[:, :-2, 1:-1] - centre)
            + face_down * (padded[:, 2:, 1:-1] - centre)
            + face_left * (padded[:, 1:-1, :-2] - centre)
            + face_right * (padded[:, 1:-1, 2:] - centre)
        )
    return values


def sweeps(values, coeffs):
    rows = values.shape[1]
    done = sweep_steps(neighbours(values, "col", 1, 1), coeffs, NSWEEP)
    return done[:, rows : 2 * rows]


def global_sum(values):
    axes = ("mem", "col")
    count = lax.axis_size(axes)
    spread = jnp.broadcast_to(values[None], (count,) + values.shape)
    return jnp.sum(lax.all_to_all(spread, axes, 0, 0, tiled=True), axis=0)


def local_inner(first, second):
    return jnp.sum(first[0] * second[0]) + jnp.sum(first[1] * second[1])


def shards(
    perturbations,
    static_root,
    obs_jacobian,
    innovations,
    obs_weights,
    length_scale,
    obs_owner,
    obs_cell,
    obs_count,
):
    members, rows_here, columns, features = perturbations.shape
    parts = lax.axis_size("mem")
    quarter = columns // parts
    offset = lax.axis_index("mem") * quarter
    blocks = lax.axis_size("col")
    obs_dev, channels = innovations.shape
    capacity = max(2, 2 * obs_dev // blocks)
    total_slots = blocks * capacity
    coeffs_wide = face_coefficients(length_scale, 2)
    coeffs = tuple(face[rows_here : 4 * rows_here] for face in coeffs_wide)
    is_live = jnp.arange(obs_dev, dtype=jnp.int32) < obs_count[0]
    owner_ids = obs_owner[:, 0]
    onehot = (
        (owner_ids[:, None] == jnp.arange(blocks, dtype=jnp.int32)[None, :]) & is_live[:, None]
    ).astype(jnp.int32)
    slot_rank = jnp.sum((jnp.cumsum(onehot, axis=0) - onehot) * onehot, axis=1)
    slot_ids = jnp.where(is_live, owner_ids * capacity + slot_rank, total_slots)
    send_values = (
        jnp.zeros((total_slots, channels), jnp.float32).at[slot_ids].set(innovations, mode="drop")
    )
    tags = jnp.stack([obs_cell.astype(jnp.float32), jnp.ones((obs_dev,), jnp.float32)], axis=1)
    tags = jnp.zeros((total_slots, 2), jnp.float32).at[slot_ids].set(tags, mode="drop")
    side = jnp.concatenate(
        [
            jnp.swapaxes(tags.reshape(blocks, capacity, 2), 1, 2).reshape(blocks, 2 * capacity),
            jnp.zeros((blocks, channels - 2 * capacity), jnp.float32),
        ],
        axis=1,
    )[:, None, :]
    packed = jnp.concatenate([send_values.reshape(blocks, capacity, channels), side], axis=1)
    got = lax.all_to_all(packed, "col", split_axis=0, concat_axis=0, tiled=True)
    got_values = got[:, :capacity, :].reshape(total_slots, channels)
    got_cells = got[:, capacity, :capacity].reshape(total_slots).astype(jnp.int32)
    got_marks = got[:, capacity, capacity : 2 * capacity].reshape(total_slots)
    obs_index = got_cells
    obs_gain = got_marks[:, None] * obs_weights[None, :]

    placement = (
        obs_index[None, :] == jnp.arange(rows_here * columns, dtype=jnp.int32)[:, None]
    ).astype(jnp.float32)

    def spread_back(weighted):
        back = jnp.dot(weighted, obs_jacobian.T, precision=lax.Precision.HIGHEST)
        grid = jnp.dot(placement, back, precision=lax.Precision.HIGHEST)
        return grid.reshape(rows_here, columns, features)

    def adjoint_parts(gradient):
        own_gradient = lax.dynamic_slice_in_dim(gradient, offset, quarter, 1)
        rounded = gradient.astype(jnp.bfloat16)
        static = jnp.dot(
            own_gradient.reshape(rows_here * quarter, features),
            static_root.T,
            precision=lax.Precision.HIGHEST,
        ).reshape(rows_here, quarter, features)
        projected = jnp.einsum(
            "kyxf,yxf->kyx", perturbations, rounded, preferred_element_type=jnp.float32
        )
        return static, projected

    def forward_partial(static_part, smoothed_field):
        smoothed = smoothed_field.astype(jnp.bfloat16)
        partial_sum = jnp.einsum(
            "kyxf,kyx->yxf", perturbations, smoothed, preferred_element_type=jnp.float32
        )
        forward_static = jnp.dot(
            static_part.reshape(rows_here * quarter, features),
            static_root,
            precision=lax.Precision.HIGHEST,
        ).reshape(rows_here, quarter, features)
        own_slice = lax.dynamic_slice_in_dim(partial_sum, offset, quarter, 1) + forward_static
        return lax.dynamic_update_slice_in_dim(partial_sum, own_slice, offset, 1)

    cell_x = obs_index % columns
    in_quarter = (cell_x >= offset) & (cell_x < offset + quarter)
    quarter_index = jnp.where(in_quarter, (obs_index // columns) * quarter + cell_x - offset, 0)
    quarter_gain = jnp.where(in_quarter[:, None], obs_gain, 0.0)
    quarter_placement = (
        (quarter_index[None, :] == jnp.arange(rows_here * quarter, dtype=jnp.int32)[:, None])
        & in_quarter[None, :]
    ).astype(jnp.float32)

    def observed(partial_sum):
        pieces = jnp.moveaxis(partial_sum.reshape(rows_here, parts, quarter, features), 1, 0)
        own_image = jnp.sum(lax.all_to_all(pieces, "mem", 0, 0, tiled=True), axis=0)
        gathered = own_image.reshape(rows_here * quarter, features)[quarter_index]
        model_obs = jnp.dot(gathered, obs_jacobian, precision=lax.Precision.HIGHEST)
        return own_image, model_obs

    def observed_adjoint(model_obs):
        back = jnp.dot(quarter_gain * model_obs, obs_jacobian.T, precision=lax.Precision.HIGHEST)
        own_gradient = jnp.dot(quarter_placement, back, precision=lax.Precision.HIGHEST)
        static = jnp.dot(own_gradient, static_root.T, precision=lax.Precision.HIGHEST).reshape(
            rows_here, quarter, features
        )
        rounded = own_gradient.reshape(rows_here, quarter, features).astype(jnp.bfloat16)
        spread = jnp.broadcast_to(rounded[None], (parts,) + rounded.shape)
        quarters = lax.all_to_all(spread, "mem", 0, 0, tiled=True)
        rounded = jnp.moveaxis(quarters, 0, 1).reshape(rows_here, columns, features)
        projected = jnp.einsum(
            "kyxf,yxf->kyx", perturbations, rounded, preferred_element_type=jnp.float32
        )
        return static, projected

    right_static, right_projected = adjoint_parts(spread_back(obs_gain * got_values))
    right_ensemble = sweeps(right_projected, coeffs)
    smoothed_right = sweeps(right_ensemble, coeffs)
    direction = (right_static, right_ensemble)

    partial0 = forward_partial(right_static, smoothed_right)
    own_image0, model_obs = observed(partial0)
    adj_static, adj_projected = observed_adjoint(model_obs)
    image = (right_static + adj_static, right_ensemble + sweeps(adj_projected, coeffs))
    sums = global_sum(
        jnp.stack(
            [
                local_inner(direction, direction),
                local_inner(direction, image),
                local_inner(image, image),
            ]
        )
    )
    smoothed_image = sweeps(image[1], coeffs)
    norm_now, curve, image_norm = sums[0], sums[1], sums[2]
    step0 = norm_now / curve
    state = (step0 * direction[0], step0 * direction[1])
    residual = (direction[0] - step0 * image[0], direction[1] - step0 * image[1])
    norm_next = norm_now - 2.0 * step0 * curve + step0 * step0 * image_norm
    ratio = norm_next / norm_now
    direction = (residual[0] + ratio * direction[0], residual[1] + ratio * direction[1])
    smoothed_direction = (smoothed_right - step0 * smoothed_image) + ratio * smoothed_right
    norm_now = norm_next

    partial1 = forward_partial(direction[0], smoothed_direction)
    own_image1, model_obs = observed(partial1)
    curve = (
        jnp.sum(direction[0] * direction[0])
        + jnp.sum(direction[1] * direction[1])
        + jnp.sum(quarter_gain * model_obs * model_obs)
    )
    step1 = norm_now / global_sum(curve)
    state = (state[0] + step1 * direction[0], state[1] + step1 * direction[1])

    increment = step0 * own_image0 + step1 * own_image1
    return (increment, state[0], state[1])


def solution(mesh):
    placed = (
        P("mem", "col", None, None),
        P(),
        P(),
        P("col", None),
        P(),
        P("col", None),
        P("col", None),
        P("col"),
        P("col"),
    )
    return jax.shard_map(
        shards,
        mesh=mesh,
        in_specs=placed,
        out_specs=(P("col", "mem", None), P("col", "mem", None), P("mem", "col", None)),
        check_vma=False,
    )
```

```python
import jax
import jax.numpy as jnp
from jax import lax
from jax.sharding import PartitionSpec as P

NSWEEP = 4
ITERS = 2


def neighbours(block, axis, dim, reach):
    count = lax.axis_size(axis)
    below, above = [], []
    for shift in range(1, reach + 1):
        forward = [(i, i + shift) for i in range(count - shift)]
        backward = [(target, source) for source, target in forward]
        below.insert(0, lax.ppermute(block, axis, forward))
        above.append(lax.ppermute(block, axis, backward))
    return jnp.concatenate(below + [block] + above, axis=dim)


def face_coefficients(length_scale, reach):
    rimmed = neighbours(length_scale, "col", 0, reach)
    padded = jnp.pad(rimmed, ((1, 1), (1, 1)))
    centre = padded[1:-1, 1:-1]
    return (
        jnp.sqrt(centre * padded[:-2, 1:-1]),
        jnp.sqrt(centre * padded[2:, 1:-1]),
        jnp.sqrt(centre * padded[1:-1, :-2]),
        jnp.sqrt(centre * padded[1:-1, 2:]),
    )


def sweep_steps(values, coeffs, count):
    face_up, face_down, face_left, face_right = coeffs
    for sweep_step in range(count):
        padded = jnp.pad(values, ((0, 0), (1, 1), (1, 1)))
        centre = values
        values = (
            centre
            + face_up * (padded[:, :-2, 1:-1] - centre)
            + face_down * (padded[:, 2:, 1:-1] - centre)
            + face_left * (padded[:, 1:-1, :-2] - centre)
            + face_right * (padded[:, 1:-1, 2:] - centre)
        )
    return values


def sweeps(values, coeffs):
    rows = values.shape[1]
    done = sweep_steps(neighbours(values, "col", 1, 1), coeffs, NSWEEP)
    return done[:, rows : 2 * rows]


def global_sum(values):
    axes = ("mem", "col")
    count = lax.axis_size(axes)
    spread = jnp.broadcast_to(values[None], (count,) + values.shape)
    return jnp.sum(lax.all_to_all(spread, axes, 0, 0, tiled=True), axis=0)


def local_inner(first, second):
    return jnp.sum(first[0] * second[0]) + jnp.sum(first[1] * second[1])


def shards(
    perturbations,
    static_root,
    obs_jacobian,
    innovations,
    obs_weights,
    length_scale,
    obs_owner,
    obs_cell,
    obs_count,
):
    members, rows_here, columns, features = perturbations.shape
    parts = lax.axis_size("mem")
    quarter = columns // parts
    offset = lax.axis_index("mem") * quarter
    blocks = lax.axis_size("col")
    obs_dev, channels = innovations.shape
    capacity = max(2, 2 * obs_dev // blocks)
    total_slots = blocks * capacity
    coeffs = face_coefficients(length_scale, 1)
    is_live = jnp.arange(obs_dev, dtype=jnp.int32) < obs_count[0]
    owner_ids = obs_owner[:, 0]
    onehot = (
        (owner_ids[:, None] == jnp.arange(blocks, dtype=jnp.int32)[None, :]) & is_live[:, None]
    ).astype(jnp.int32)
    slot_rank = jnp.sum((jnp.cumsum(onehot, axis=0) - onehot) * onehot, axis=1)
    slot_ids = jnp.where(is_live, owner_ids * capacity + slot_rank, total_slots)
    send_values = (
        jnp.zeros((total_slots, channels), jnp.float32).at[slot_ids].set(innovations, mode="drop")
    )
    tags = jnp.stack([obs_cell.astype(jnp.float32), jnp.ones((obs_dev,), jnp.float32)], axis=1)
    tags = jnp.zeros((total_slots, 2), jnp.float32).at[slot_ids].set(tags, mode="drop")
    side = jnp.concatenate(
        [
            jnp.swapaxes(tags.reshape(blocks, capacity, 2), 1, 2).reshape(blocks, 2 * capacity),
            jnp.zeros((blocks, channels - 2 * capacity), jnp.float32),
        ],
        axis=1,
    )[:, None, :]
    packed = jnp.concatenate([send_values.reshape(blocks, capacity, channels), side], axis=1)
    got = lax.all_to_all(packed, "col", split_axis=0, concat_axis=0, tiled=True)
    got_values = got[:, :capacity, :].reshape(total_slots, channels)
    got_cells = got[:, capacity, :capacity].reshape(total_slots).astype(jnp.int32)
    got_marks = got[:, capacity, capacity : 2 * capacity].reshape(total_slots)
    obs_index = got_cells
    obs_gain = got_marks[:, None] * obs_weights[None, :]

    placement = (
        obs_index[None, :] == jnp.arange(rows_here * columns, dtype=jnp.int32)[:, None]
    ).astype(jnp.float32)

    def spread_back(weighted):
        back = jnp.dot(weighted, obs_jacobian.T, precision=lax.Precision.HIGHEST)
        grid = jnp.dot(placement, back, precision=lax.Precision.HIGHEST)
        return grid.reshape(rows_here, columns, features)

    def adjoint_parts(gradient):
        own_gradient = lax.dynamic_slice_in_dim(gradient, offset, quarter, 1)
        rounded = gradient.astype(jnp.bfloat16)
        static = jnp.dot(
            own_gradient.reshape(rows_here * quarter, features),
            static_root.T,
            precision=lax.Precision.HIGHEST,
        ).reshape(rows_here, quarter, features)
        projected = jnp.einsum(
            "kyxf,yxf->kyx", perturbations, rounded, preferred_element_type=jnp.float32
        )
        return static, projected

    def forward_partial(static_part, smoothed_field):
        smoothed = smoothed_field.astype(jnp.bfloat16)
        partial_sum = jnp.einsum(
            "kyxf,kyx->yxf", perturbations, smoothed, preferred_element_type=jnp.float32
        )
        forward_static = jnp.dot(
            static_part.reshape(rows_here * quarter, features),
            static_root,
            precision=lax.Precision.HIGHEST,
        ).reshape(rows_here, quarter, features)
        own_slice = lax.dynamic_slice_in_dim(partial_sum, offset, quarter, 1) + forward_static
        return lax.dynamic_update_slice_in_dim(partial_sum, own_slice, offset, 1)

    cell_x = obs_index % columns
    in_quarter = (cell_x >= offset) & (cell_x < offset + quarter)
    quarter_index = jnp.where(in_quarter, (obs_index // columns) * quarter + cell_x - offset, 0)
    quarter_gain = jnp.where(in_quarter[:, None], obs_gain, 0.0)
    quarter_placement = (
        (quarter_index[None, :] == jnp.arange(rows_here * quarter, dtype=jnp.int32)[:, None])
        & in_quarter[None, :]
    ).astype(jnp.float32)

    def observed(partial_sum):
        pieces = jnp.moveaxis(partial_sum.reshape(rows_here, parts, quarter, features), 1, 0)
        own_image = jnp.sum(lax.all_to_all(pieces, "mem", 0, 0, tiled=True), axis=0)
        gathered = own_image.reshape(rows_here * quarter, features)[quarter_index]
        model_obs = jnp.dot(gathered, obs_jacobian, precision=lax.Precision.HIGHEST)
        return own_image, model_obs

    def observed_adjoint(model_obs):
        back = jnp.dot(quarter_gain * model_obs, obs_jacobian.T, precision=lax.Precision.HIGHEST)
        own_gradient = jnp.dot(quarter_placement, back, precision=lax.Precision.HIGHEST)
        static = jnp.dot(own_gradient, static_root.T, precision=lax.Precision.HIGHEST).reshape(
            rows_here, quarter, features
        )
        rounded = own_gradient.reshape(rows_here, quarter, features).astype(jnp.bfloat16)
        spread = jnp.broadcast_to(rounded[None], (parts,) + rounded.shape)
        quarters = lax.all_to_all(spread, "mem", 0, 0, tiled=True)
        rounded = jnp.moveaxis(quarters, 0, 1).reshape(rows_here, columns, features)
        projected = jnp.einsum(
            "kyxf,yxf->kyx", perturbations, rounded, preferred_element_type=jnp.float32
        )
        return static, projected

    right_static, right_projected = adjoint_parts(spread_back(obs_gain * got_values))
    right_ensemble = sweeps(right_projected, coeffs)
    smoothed_right = sweeps(right_ensemble, coeffs)
    direction = (right_static, right_ensemble)

    partial0 = forward_partial(right_static, smoothed_right)
    own_image0, model_obs = observed(partial0)
    adj_static, adj_projected = observed_adjoint(model_obs)
    image = (right_static + adj_static, right_ensemble + sweeps(adj_projected, coeffs))
    sums = global_sum(
        jnp.stack(
            [
                local_inner(direction, direction),
                local_inner(direction, image),
                local_inner(image, image),
            ]
        )
    )
    smoothed_image = sweeps(image[1], coeffs)
    norm_now, curve, image_norm = sums[0], sums[1], sums[2]
    step0 = norm_now / curve
    state = (step0 * direction[0], step0 * direction[1])
    residual = (direction[0] - step0 * image[0], direction[1] - step0 * image[1])
    norm_next = norm_now - 2.0 * step0 * curve + step0 * step0 * image_norm
    ratio = norm_next / norm_now
    direction = (residual[0] + ratio * direction[0], residual[1] + ratio * direction[1])
    smoothed_direction = (smoothed_right - step0 * smoothed_image) + ratio * smoothed_right
    norm_now = norm_next

    partial1 = forward_partial(direction[0], smoothed_direction)
    own_image1, model_obs = observed(partial1)
    curve = (
        jnp.sum(direction[0] * direction[0])
        + jnp.sum(direction[1] * direction[1])
        + jnp.sum(quarter_gain * model_obs * model_obs)
    )
    step1 = norm_now / global_sum(curve)
    state = (state[0] + step1 * direction[0], state[1] + step1 * direction[1])

    increment = step0 * own_image0 + step1 * own_image1
    return (increment, state[0], state[1])


def solution(mesh):
    placed = (
        P("mem", "col", None, None),
        P(),
        P(),
        P("col", None),
        P(),
        P("col", None),
        P("col", None),
        P("col"),
        P("col"),
    )
    return jax.shard_map(
        shards,
        mesh=mesh,
        in_specs=placed,
        out_specs=(P("col", "mem", None), P("col", "mem", None), P("mem", "col", None)),
        check_vma=False,
    )
```

```python
import jax
import jax.numpy as jnp
from jax import lax
from jax.sharding import PartitionSpec as P

NSWEEP = 4
ITERS = 2


def neighbours(block, axis, dim, reach):
    count = lax.axis_size(axis)
    below, above = [], []
    for shift in range(1, reach + 1):
        forward = [(i, i + shift) for i in range(count - shift)]
        backward = [(target, source) for source, target in forward]
        below.insert(0, lax.ppermute(block, axis, forward))
        above.append(lax.ppermute(block, axis, backward))
    return jnp.concatenate(below + [block] + above, axis=dim)


def face_coefficients(length_scale, reach):
    rimmed = neighbours(length_scale, "col", 0, reach)
    padded = jnp.pad(rimmed, ((1, 1), (1, 1)))
    centre = padded[1:-1, 1:-1]
    return (
        jnp.sqrt(centre * padded[:-2, 1:-1]),
        jnp.sqrt(centre * padded[2:, 1:-1]),
        jnp.sqrt(centre * padded[1:-1, :-2]),
        jnp.sqrt(centre * padded[1:-1, 2:]),
    )


def sweep_steps(values, coeffs, count):
    face_up, face_down, face_left, face_right = coeffs
    for sweep_step in range(count):
        padded = jnp.pad(values, ((0, 0), (1, 1), (1, 1)))
        centre = values
        values = (
            centre
            + face_up * (padded[:, :-2, 1:-1] - centre)
            + face_down * (padded[:, 2:, 1:-1] - centre)
            + face_left * (padded[:, 1:-1, :-2] - centre)
            + face_right * (padded[:, 1:-1, 2:] - centre)
        )
    return values


def sweeps(values, coeffs):
    rows = values.shape[1]
    done = sweep_steps(neighbours(values, "col", 1, 1), coeffs, NSWEEP)
    return done[:, rows : 2 * rows]


def global_sum(values):
    axes = ("mem", "col")
    count = lax.axis_size(axes)
    spread = jnp.broadcast_to(values[None], (count,) + values.shape)
    return jnp.sum(lax.all_to_all(spread, axes, 0, 0, tiled=True), axis=0)


def local_inner(first, second):
    return jnp.sum(first[0] * second[0]) + jnp.sum(first[1] * second[1])


def shards(
    perturbations,
    static_root,
    obs_jacobian,
    innovations,
    obs_weights,
    length_scale,
    obs_owner,
    obs_cell,
    obs_count,
):
    members, rows_here, columns, features = perturbations.shape
    parts = lax.axis_size("mem")
    quarter = columns // parts
    offset = lax.axis_index("mem") * quarter
    blocks = lax.axis_size("col")
    obs_dev, channels = innovations.shape
    capacity = max(2, 2 * obs_dev // blocks)
    total_slots = blocks * capacity
    coeffs = face_coefficients(length_scale, 1)
    is_live = jnp.arange(obs_dev, dtype=jnp.int32) < obs_count[0]
    owner_ids = obs_owner[:, 0]
    onehot = (
        (owner_ids[:, None] == jnp.arange(blocks, dtype=jnp.int32)[None, :]) & is_live[:, None]
    ).astype(jnp.int32)
    slot_rank = jnp.sum((jnp.cumsum(onehot, axis=0) - onehot) * onehot, axis=1)
    slot_ids = jnp.where(is_live, owner_ids * capacity + slot_rank, total_slots)
    send_values = (
        jnp.zeros((total_slots, channels), jnp.float32).at[slot_ids].set(innovations, mode="drop")
    )
    tags = jnp.stack([obs_cell.astype(jnp.float32), jnp.ones((obs_dev,), jnp.float32)], axis=1)
    tags = jnp.zeros((total_slots, 2), jnp.float32).at[slot_ids].set(tags, mode="drop")
    side = jnp.concatenate(
        [
            jnp.swapaxes(tags.reshape(blocks, capacity, 2), 1, 2).reshape(blocks, 2 * capacity),
            jnp.zeros((blocks, channels - 2 * capacity), jnp.float32),
        ],
        axis=1,
    )[:, None, :]
    packed = jnp.concatenate([send_values.reshape(blocks, capacity, channels), side], axis=1)
    got = lax.all_to_all(packed, "col", split_axis=0, concat_axis=0, tiled=True)
    got_values = got[:, :capacity, :].reshape(total_slots, channels)
    got_cells = got[:, capacity, :capacity].reshape(total_slots).astype(jnp.int32)
    got_marks = got[:, capacity, capacity : 2 * capacity].reshape(total_slots)
    obs_index = got_cells
    obs_gain = got_marks[:, None] * obs_weights[None, :]

    placement = (
        obs_index[None, :] == jnp.arange(rows_here * columns, dtype=jnp.int32)[:, None]
    ).astype(jnp.float32)

    def spread_back(weighted):
        back = jnp.dot(weighted, obs_jacobian.T, precision=lax.Precision.HIGHEST)
        grid = jnp.dot(placement, back, precision=lax.Precision.HIGHEST)
        return grid.reshape(rows_here, columns, features)

    def adjoint_parts(gradient):
        own_gradient = lax.dynamic_slice_in_dim(gradient, offset, quarter, 1)
        rounded = gradient.astype(jnp.bfloat16)
        static = jnp.dot(
            own_gradient.reshape(rows_here * quarter, features),
            static_root.T,
            precision=lax.Precision.HIGHEST,
        ).reshape(rows_here, quarter, features)
        projected = jnp.einsum(
            "kyxf,yxf->kyx", perturbations, rounded, preferred_element_type=jnp.float32
        )
        return static, projected

    def forward_partial(static_part, smoothed_field):
        smoothed = smoothed_field.astype(jnp.bfloat16)
        partial_sum = jnp.einsum(
            "kyxf,kyx->yxf", perturbations, smoothed, preferred_element_type=jnp.float32
        )
        forward_static = jnp.dot(
            static_part.reshape(rows_here * quarter, features),
            static_root,
            precision=lax.Precision.HIGHEST,
        ).reshape(rows_here, quarter, features)
        own_slice = lax.dynamic_slice_in_dim(partial_sum, offset, quarter, 1) + forward_static
        return lax.dynamic_update_slice_in_dim(partial_sum, own_slice, offset, 1)

    cell_x = obs_index % columns
    in_quarter = (cell_x >= offset) & (cell_x < offset + quarter)
    quarter_index = jnp.where(in_quarter, (obs_index // columns) * quarter + cell_x - offset, 0)
    quarter_gain = jnp.where(in_quarter[:, None], obs_gain, 0.0)
    quarter_placement = (
        (quarter_index[None, :] == jnp.arange(rows_here * quarter, dtype=jnp.int32)[:, None])
        & in_quarter[None, :]
    ).astype(jnp.float32)

    def observed(partial_sum):
        pieces = jnp.moveaxis(partial_sum.reshape(rows_here, parts, quarter, features), 1, 0)
        own_image = jnp.sum(lax.all_to_all(pieces, "mem", 0, 0, tiled=True), axis=0)
        gathered = jnp.dot(
            quarter_placement.T,
            own_image.reshape(rows_here * quarter, features),
            precision=lax.Precision.HIGHEST,
        )
        model_obs = jnp.dot(gathered, obs_jacobian, precision=lax.Precision.HIGHEST)
        return own_image, model_obs

    def observed_adjoint(model_obs):
        back = jnp.dot(quarter_gain * model_obs, obs_jacobian.T, precision=lax.Precision.HIGHEST)
        own_gradient = jnp.dot(quarter_placement, back, precision=lax.Precision.HIGHEST)
        static = jnp.dot(own_gradient, static_root.T, precision=lax.Precision.HIGHEST).reshape(
            rows_here, quarter, features
        )
        rounded = own_gradient.reshape(rows_here, quarter, features).astype(jnp.bfloat16)
        spread = jnp.broadcast_to(rounded[None], (parts,) + rounded.shape)
        quarters = lax.all_to_all(spread, "mem", 0, 0, tiled=True)
        rounded = jnp.moveaxis(quarters, 0, 1).reshape(rows_here, columns, features)
        projected = jnp.einsum(
            "kyxf,yxf->kyx", perturbations, rounded, preferred_element_type=jnp.float32
        )
        return static, projected

    right_static, right_projected = adjoint_parts(spread_back(obs_gain * got_values))
    right_ensemble = sweeps(right_projected, coeffs)
    smoothed_right = sweeps(right_ensemble, coeffs)
    direction = (right_static, right_ensemble)

    partial0 = forward_partial(right_static, smoothed_right)
    own_image0, model_obs = observed(partial0)
    adj_static, adj_projected = observed_adjoint(model_obs)
    image = (right_static + adj_static, right_ensemble + sweeps(adj_projected, coeffs))
    sums = global_sum(
        jnp.stack(
            [
                local_inner(direction, direction),
                local_inner(direction, image),
                local_inner(image, image),
            ]
        )
    )
    smoothed_image = sweeps(image[1], coeffs)
    norm_now, curve, image_norm = sums[0], sums[1], sums[2]
    step0 = norm_now / curve
    state = (step0 * direction[0], step0 * direction[1])
    residual = (direction[0] - step0 * image[0], direction[1] - step0 * image[1])
    norm_next = norm_now - 2.0 * step0 * curve + step0 * step0 * image_norm
    ratio = norm_next / norm_now
    direction = (residual[0] + ratio * direction[0], residual[1] + ratio * direction[1])
    smoothed_direction = (smoothed_right - step0 * smoothed_image) + ratio * smoothed_right
    norm_now = norm_next

    partial1 = forward_partial(direction[0], smoothed_direction)
    own_image1, model_obs = observed(partial1)
    curve = (
        jnp.sum(direction[0] * direction[0])
        + jnp.sum(direction[1] * direction[1])
        + jnp.sum(quarter_gain * model_obs * model_obs)
    )
    step1 = norm_now / global_sum(curve)
    state = (state[0] + step1 * direction[0], state[1] + step1 * direction[1])

    increment = step0 * own_image0 + step1 * own_image1
    return (increment, state[0], state[1])


def solution(mesh):
    placed = (
        P("mem", "col", None, None),
        P(),
        P(),
        P("col", None),
        P(),
        P("col", None),
        P("col", None),
        P("col"),
        P("col"),
    )
    return jax.shard_map(
        shards,
        mesh=mesh,
        in_specs=placed,
        out_specs=(P("col", "mem", None), P("col", "mem", None), P("mem", "col", None)),
        check_vma=False,
    )
```

```python
import jax
import jax.numpy as jnp
from jax import lax
from jax.sharding import PartitionSpec as P

NSWEEP = 4
ITERS = 2


def neighbours(block, axis, dim, reach):
    count = lax.axis_size(axis)
    below, above = [], []
    for shift in range(1, reach + 1):
        forward = [(i, i + shift) for i in range(count - shift)]
        backward = [(target, source) for source, target in forward]
        below.insert(0, lax.ppermute(block, axis, forward))
        above.append(lax.ppermute(block, axis, backward))
    return jnp.concatenate(below + [block] + above, axis=dim)


def face_coefficients(length_scale, reach):
    rimmed = neighbours(length_scale, "col", 0, reach)
    padded = jnp.pad(rimmed, ((1, 1), (1, 1)))
    centre = padded[1:-1, 1:-1]
    return (
        jnp.sqrt(centre * padded[:-2, 1:-1]),
        jnp.sqrt(centre * padded[2:, 1:-1]),
        jnp.sqrt(centre * padded[1:-1, :-2]),
        jnp.sqrt(centre * padded[1:-1, 2:]),
    )


def sweep_steps(values, coeffs, count):
    face_up, face_down, face_left, face_right = coeffs
    for sweep_step in range(count):
        padded = jnp.pad(values, ((0, 0), (1, 1), (1, 1)))
        centre = values
        values = (
            centre
            + face_up * (padded[:, :-2, 1:-1] - centre)
            + face_down * (padded[:, 2:, 1:-1] - centre)
            + face_left * (padded[:, 1:-1, :-2] - centre)
            + face_right * (padded[:, 1:-1, 2:] - centre)
        )
    return values


def sweeps(values, coeffs):
    rows = values.shape[1]
    done = sweep_steps(neighbours(values, "col", 1, 1), coeffs, NSWEEP)
    return done[:, rows : 2 * rows]


def global_sum(values):
    axes = ("mem", "col")
    count = lax.axis_size(axes)
    spread = jnp.broadcast_to(values[None], (count,) + values.shape)
    return jnp.sum(lax.all_to_all(spread, axes, 0, 0, tiled=True), axis=0)


def local_inner(first, second):
    return jnp.sum(first[0] * second[0]) + jnp.sum(first[1] * second[1])


def shards(
    perturbations,
    static_root,
    obs_jacobian,
    innovations,
    obs_weights,
    length_scale,
    obs_owner,
    obs_cell,
    obs_count,
):
    members, rows_here, columns, features = perturbations.shape
    parts = lax.axis_size("mem")
    quarter = columns // parts
    offset = lax.axis_index("mem") * quarter
    blocks = lax.axis_size("col")
    obs_dev, channels = innovations.shape
    capacity = max(2, 2 * obs_dev // blocks)
    total_slots = blocks * capacity
    coeffs = face_coefficients(length_scale, 1)
    is_live = jnp.arange(obs_dev, dtype=jnp.int32) < obs_count[0]
    owner_ids = obs_owner[:, 0]
    onehot = (
        (owner_ids[:, None] == jnp.arange(blocks, dtype=jnp.int32)[None, :]) & is_live[:, None]
    ).astype(jnp.int32)
    slot_rank = jnp.sum((jnp.cumsum(onehot, axis=0) - onehot) * onehot, axis=1)
    slot_ids = jnp.where(is_live, owner_ids * capacity + slot_rank, total_slots)
    send_values = (
        jnp.zeros((total_slots, channels), jnp.float32).at[slot_ids].set(innovations, mode="drop")
    )
    tags = jnp.stack([obs_cell.astype(jnp.float32), jnp.ones((obs_dev,), jnp.float32)], axis=1)
    tags = jnp.zeros((total_slots, 2), jnp.float32).at[slot_ids].set(tags, mode="drop")
    side = jnp.concatenate(
        [
            jnp.swapaxes(tags.reshape(blocks, capacity, 2), 1, 2).reshape(blocks, 2 * capacity),
            jnp.zeros((blocks, channels - 2 * capacity), jnp.float32),
        ],
        axis=1,
    )[:, None, :]
    packed = jnp.concatenate([send_values.reshape(blocks, capacity, channels), side], axis=1)
    got = lax.all_to_all(packed, "col", split_axis=0, concat_axis=0, tiled=True)
    got_values = got[:, :capacity, :].reshape(total_slots, channels)
    got_cells = got[:, capacity, :capacity].reshape(total_slots).astype(jnp.int32)
    got_marks = got[:, capacity, capacity : 2 * capacity].reshape(total_slots)
    obs_index = got_cells
    obs_gain = got_marks[:, None] * obs_weights[None, :]

    placement = (
        obs_index[None, :] == jnp.arange(rows_here * columns, dtype=jnp.int32)[:, None]
    ).astype(jnp.float32)

    def spread_back(weighted):
        back = jnp.dot(weighted, obs_jacobian.T, precision=lax.Precision.HIGHEST)
        grid = jnp.dot(placement, back, precision=lax.Precision.HIGHEST)
        return grid.reshape(rows_here, columns, features)

    def adjoint_parts(gradient):
        own_gradient = lax.dynamic_slice_in_dim(gradient, offset, quarter, 1)
        rounded = gradient.astype(jnp.bfloat16)
        static = jnp.dot(
            own_gradient.reshape(rows_here * quarter, features),
            static_root.T,
            precision=lax.Precision.HIGHEST,
        ).reshape(rows_here, quarter, features)
        projected = jnp.einsum(
            "kyxf,yxf->kyx", perturbations, rounded, preferred_element_type=jnp.float32
        )
        return static, projected

    def forward_partial(static_part, smoothed_field):
        smoothed = smoothed_field.astype(jnp.bfloat16)
        partial_sum = jnp.einsum(
            "kyxf,kyx->yxf", perturbations, smoothed, preferred_element_type=jnp.float32
        )
        forward_static = jnp.dot(
            static_part.reshape(rows_here * quarter, features),
            static_root,
            precision=lax.Precision.HIGHEST,
        ).reshape(rows_here, quarter, features)
        return partial_sum, forward_static

    cell_x = obs_index % columns
    in_quarter = (cell_x >= offset) & (cell_x < offset + quarter)
    quarter_index = jnp.where(in_quarter, (obs_index // columns) * quarter + cell_x - offset, 0)
    quarter_gain = jnp.where(in_quarter[:, None], obs_gain, 0.0)
    quarter_placement = (
        (quarter_index[None, :] == jnp.arange(rows_here * quarter, dtype=jnp.int32)[:, None])
        & in_quarter[None, :]
    ).astype(jnp.float32)

    def observed(parts_of_image):
        partial_sum, forward_static = parts_of_image
        pieces = jnp.moveaxis(partial_sum.reshape(rows_here, parts, quarter, features), 1, 0)
        own_image = jnp.sum(lax.all_to_all(pieces, "mem", 0, 0, tiled=True), axis=0) + forward_static
        gathered = jnp.dot(
            quarter_placement.T,
            own_image.reshape(rows_here * quarter, features),
            precision=lax.Precision.HIGHEST,
        )
        model_obs = jnp.dot(gathered, obs_jacobian, precision=lax.Precision.HIGHEST)
        return own_image, model_obs

    def observed_adjoint(model_obs):
        back = jnp.dot(quarter_gain * model_obs, obs_jacobian.T, precision=lax.Precision.HIGHEST)
        own_gradient = jnp.dot(quarter_placement, back, precision=lax.Precision.HIGHEST)
        static = jnp.dot(own_gradient, static_root.T, precision=lax.Precision.HIGHEST).reshape(
            rows_here, quarter, features
        )
        rounded = own_gradient.reshape(rows_here, quarter, features).astype(jnp.bfloat16)
        spread = jnp.broadcast_to(rounded[None], (parts,) + rounded.shape)
        quarters = lax.all_to_all(spread, "mem", 0, 0, tiled=True)
        rounded = jnp.moveaxis(quarters, 0, 1).reshape(rows_here, columns, features)
        projected = jnp.einsum(
            "kyxf,yxf->kyx", perturbations, rounded, preferred_element_type=jnp.float32
        )
        return static, projected

    right_static, right_projected = adjoint_parts(spread_back(obs_gain * got_values))
    right_ensemble = sweeps(right_projected, coeffs)
    smoothed_right = sweeps(right_ensemble, coeffs)
    direction = (right_static, right_ensemble)

    partial0 = forward_partial(right_static, smoothed_right)
    own_image0, model_obs = observed(partial0)
    adj_static, adj_projected = observed_adjoint(model_obs)
    image = (right_static + adj_static, right_ensemble + sweeps(adj_projected, coeffs))
    sums = global_sum(
        jnp.stack(
            [
                local_inner(direction, direction),
                local_inner(direction, image),
                local_inner(image, image),
            ]
        )
    )
    smoothed_image = sweeps(image[1], coeffs)
    norm_now, curve, image_norm = sums[0], sums[1], sums[2]
    step0 = norm_now / curve
    state = (step0 * direction[0], step0 * direction[1])
    residual = (direction[0] - step0 * image[0], direction[1] - step0 * image[1])
    norm_next = norm_now - 2.0 * step0 * curve + step0 * step0 * image_norm
    ratio = norm_next / norm_now
    direction = (residual[0] + ratio * direction[0], residual[1] + ratio * direction[1])
    smoothed_direction = (smoothed_right - step0 * smoothed_image) + ratio * smoothed_right
    norm_now = norm_next

    partial1 = forward_partial(direction[0], smoothed_direction)
    own_image1, model_obs = observed(partial1)
    curve = (
        jnp.sum(direction[0] * direction[0])
        + jnp.sum(direction[1] * direction[1])
        + jnp.sum(quarter_gain * model_obs * model_obs)
    )
    step1 = norm_now / global_sum(curve)
    state = (state[0] + step1 * direction[0], state[1] + step1 * direction[1])

    increment = step0 * own_image0 + step1 * own_image1
    return (increment, state[0], state[1])


def solution(mesh):
    placed = (
        P("mem", "col", None, None),
        P(),
        P(),
        P("col", None),
        P(),
        P("col", None),
        P("col", None),
        P("col"),
        P("col"),
    )
    return jax.shard_map(
        shards,
        mesh=mesh,
        in_specs=placed,
        out_specs=(P("col", "mem", None), P("col", "mem", None), P("mem", "col", None)),
        check_vma=False,
    )
```
